32 devices in a mesh: dp: 8 (over y, x, core), tensor: 4 (over z).
Axes of the slice: x: 2, y: 2, z: 4, core: 2. Of those that a mesh axis runs over, the one named last changes fastest.
Arguments:
- glu_input: bfloat16 [16, 256, 3072], P('dp', 'tensor'), may hold values from -12 to 12
- depth_kernel: float32 [31, 1536], replicated, may hold values from -1 to 1
- norm_scale: float32 [1536], replicated, may hold values from 0.5 to 1.5
- norm_shift: float32 [1536], replicated, may hold values from -3 to 3
- proj_weight: bfloat16 [1536, 1536], P('tensor'), may hold values from -0.15625 to 0.15625
- out_grad: bfloat16 [16, 256, 1536], P('dp', 'tensor'), may hold values from -6 to 6
Outputs:
- conv_output: bfloat16 [16, 256, 1536], P('dp', 'tensor')
- input_grad: bfloat16 [16, 256, 3072], P('dp', 'tensor')
- weight_grad: float32 [1536, 1536], P('tensor')
- kernel_grad: float32 [31, 1536], replicated
- scale_grad: float32 [1536], replicated
- shift_grad: float32 [1536], replicated
The draws below stay inside these ranges and needn't reach their ends.
All inputs are finite; a program needn't handle non-finite values.
Results may differ from the reference program's by a relative error of at most 0.0057.
Values may be sent and summed in bfloat16 or wider, within the bound.
No kernel may reach another device: no remote copies, remote signals or barrier semaphores. Data moves between devices by JAX's collectives and lax.ppermute only.
A program may use at most 128 MiB of HBM per device.

```python
import jax
import jax.numpy as jnp
from jax import lax

D = 1536
K = 31
BATCH = 16
LENGTH = 256


def draw_glu_input(key, part):
    key_noise, key_rough, key_channel = jax.random.split(key, 3)
    position = jnp.arange(LENGTH, dtype=jnp.float32) / LENGTH
    rising = jnp.exp(jnp.log(3.0) * position)[None, :, None]
    roughness = jax.random.uniform(key_rough, (BATCH, LENGTH, 1), jnp.float32, 0.6, 1.4)
    noise = jax.random.normal(key_noise, (BATCH, LENGTH, 2 * D), jnp.float32)
    offsets = jax.random.normal(key_channel, (1, 1, 2 * D), jnp.float32) * 0.5
    result = noise * rising * roughness + offsets
    return jnp.clip(result, -12.0, 12.0).astype(jnp.bfloat16)


def levels(own_key, shape, cuts, low, top_value):
    level = 1.0
    for axis_at, parts in cuts:
        steps = jax.random.uniform(jax.random.fold_in(jax.random.fold_in(own_key, 6), axis_at), (parts,), jnp.float32, low / len(cuts), top_value / len(cuts))
        level = level * jnp.repeat(jnp.exp(steps), shape[axis_at] // parts).reshape((-1,) + (1,) * (len(shape) - 1 - axis_at))
    return level


def scatter_about(stream_key, extent, width, most, shards=(), kind=jnp.bfloat16):
    entries = jax.random.normal(stream_key, extent, jnp.float32) * width
    if len(shards) > 0:
        entries = levels(stream_key, extent, shards, -0.22, 0.18) * entries
    return jnp.clip(entries, min=-most, max=most).astype(kind)


def setup_inputs(seed: int = 0) -> dict:
    keys = jax.random.split(jax.random.key(seed), 7)
    glu_input = draw_glu_input(jax.random.fold_in(keys[6], 71), 0)
    depth_kernel = scatter_about(keys[1], (K, D), K ** -0.5, 1.0, (), jnp.float32)
    norm_scale = jnp.clip(jax.random.uniform(keys[2], (D,), jnp.float32, 0.5, 1.5), 0.5, 1.5)
    norm_shift = scatter_about(keys[3], (D,), 0.5, 3.0, (), jnp.float32)
    proj_weight = scatter_about(keys[4], (D, D), D ** -0.5, 0.15625, ((0, 4),))
    out_grad = scatter_about(keys[5], (BATCH, LENGTH, D), 1.0, 6.0, ((0, 8), (1, 4)))
    return dict(glu_input=glu_input, depth_kernel=depth_kernel, norm_scale=norm_scale, norm_shift=norm_shift, proj_weight=proj_weight, out_grad=out_grad)


def reference(glu_input, depth_kernel, norm_scale, norm_shift, proj_weight, out_grad):
    radius = (K - 1) // 2
    frames_all = BATCH * LENGTH
    values = glu_input[..., :D].astype(jnp.float32)
    gates = jax.nn.sigmoid(glu_input[..., D:].astype(jnp.float32))
    gated = (values * gates).astype(jnp.bfloat16)
    padded = jnp.pad(gated, ((0, 0), (radius, radius), (0, 0)))
    conv_out = jnp.zeros((BATCH, LENGTH, D), jnp.float32)
    for offset in range(K):
        conv_out = conv_out + depth_kernel[offset] * padded[:, offset:offset + LENGTH, :]
    average = lax.optimization_barrier(jnp.sum(conv_out, axis=(0, 1))) / frames_all
    centred = conv_out - average
    variance = lax.optimization_barrier(jnp.sum(centred * centred, axis=(0, 1))) / frames_all
    inverse = lax.rsqrt(variance + 1e-05)
    normed = centred * inverse
    affine = norm_scale * normed + norm_shift
    sig_affine = jax.nn.sigmoid(affine)
    activated = (affine * sig_affine).astype(jnp.bfloat16)
    flat_act = activated.reshape(-1, D)
    flat_grad = out_grad.reshape(-1, D)
    conv_output = jnp.dot(flat_act, proj_weight, preferred_element_type=jnp.float32).astype(jnp.bfloat16).reshape(BATCH, LENGTH, D)
    grad_act = jnp.dot(flat_grad, proj_weight.T, preferred_element_type=jnp.float32).reshape(BATCH, LENGTH, D)
    grad_affine = grad_act * (sig_affine + affine * sig_affine * (1.0 - sig_affine))
    shift_grad = lax.optimization_barrier(jnp.sum(grad_affine, axis=(0, 1)))
    scale_grad = lax.optimization_barrier(jnp.sum(grad_affine * normed, axis=(0, 1)))
    grad_conv = (norm_scale * inverse * (grad_affine - shift_grad / frames_all - normed * scale_grad / frames_all)).astype(jnp.bfloat16)
    grad_pad = jnp.pad(grad_conv, ((0, 0), (radius, radius), (0, 0)))
    grad_gated = jnp.zeros((BATCH, LENGTH, D), jnp.float32)
    for offset in range(K):
        begin = 2 * radius - offset
        grad_gated = grad_gated + depth_kernel[offset] * grad_pad[:, begin:begin + LENGTH, :]
    grad_wide = grad_conv.astype(jnp.float32)
    kernel_grad = jnp.stack([lax.optimization_barrier(jnp.sum(padded[:, offset:offset + LENGTH, :].astype(jnp.float32) * grad_wide, axis=(0, 1))) for offset in range(K)])
    input_grad = jnp.concatenate([grad_gated * gates, grad_gated * values * gates * (1.0 - gates)], axis=-1).astype(jnp.bfloat16)
    weight_grad = jnp.dot(flat_act.T, flat_grad, preferred_element_type=jnp.float32)
    return (conv_output, input_grad, weight_grad, kernel_grad, scale_grad, shift_grad)
```

```python
import jax
import jax.numpy as jnp
from jax import lax
from jax.sharding import PartitionSpec as P

epsilon = 1e-05


def extended(array, sides, width):
    for axis, dim in sides:
        peers, length = (lax.axis_size(axis), array.shape[dim])
        up = [(i, (i + 1) % peers) for i in range(peers - 1)]
        down = [(j, i) for i, j in up]
        last = lax.slice_in_dim(array, length - width, length, axis=dim)
        leading = lax.slice_in_dim(array, 0, width, axis=dim)
        before = lax.ppermute(last, axis, up)
        after = lax.ppermute(leading, axis, down)
        array = jnp.concatenate([before, array, after], axis=dim)
    return array


def is_power_of_two(n):
    return n > 0 and (n & (n - 1)) == 0


def all_sum(x, axes):
    for axis in axes:
        peers = lax.axis_size(axis)
        if not is_power_of_two(peers):
            x = lax.psum(x, axis)
            continue
        step = 1
        while step < peers:
            x = x + lax.ppermute(x, axis, [(i, i ^ step) for i in range(peers)])
            step *= 2
    return x


def all_moments(mean, spread, count, axes):
    for axis in axes:
        peers = lax.axis_size(axis)
        step = 1
        while step < peers:
            other = lax.ppermute(jnp.stack([mean, spread]), axis, [(i, i ^ step) for i in range(peers)])
            delta = other[0] - mean
            mean = (mean + other[0]) * 0.5
            spread = (spread + other[1]) + delta * delta * (count * 0.5)
            count = count * 2
            step *= 2
    return mean, spread


def shifted(x, axis, shift):
    peers = lax.axis_size(axis)
    return lax.ppermute(x, axis, [(i, (i + shift) % peers) for i in range(peers)])


def on_device(glu_input, depth_kernel, norm_scale, norm_shift, proj_weight, out_grad):
    width = proj_weight.shape[1]
    rows = proj_weight.shape[0]
    frames = glu_input.shape[1]
    taps = depth_kernel.shape[0]
    radius = (taps - 1) // 2
    peers = lax.axis_size("tensor")
    me = lax.axis_index("tensor")
    local = glu_input.shape[0] * frames
    everyone = local * lax.axis_size("dp") * peers
    full_weight = lax.all_gather(proj_weight, "tensor", axis=0, tiled=True)
    values = glu_input[..., :width].astype(jnp.float32)
    gates = jax.nn.sigmoid(glu_input[..., width:].astype(jnp.float32))
    gated = (values * gates).astype(jnp.bfloat16)
    padded = extended(gated, (("tensor", 1),), radius)
    conv_out = jnp.zeros(gated.shape, jnp.float32)
    for offset in range(taps):
        conv_out = conv_out + depth_kernel[offset] * padded[:, offset : offset + frames, :]
    mean_local = jnp.sum(conv_out, axis=(0, 1)) / local
    dev_local = conv_out - mean_local
    spread_local = jnp.sum(dev_local * dev_local, axis=(0, 1))
    if all(is_power_of_two(lax.axis_size(a)) for a in ("dp", "tensor")):
        average, spread = all_moments(mean_local, spread_local, float(local), ("dp", "tensor"))
        variance = spread / everyone
    else:
        average = lax.psum(jnp.sum(conv_out, axis=(0, 1)), ("dp", "tensor")) / everyone
        centred0 = conv_out - average
        variance = lax.psum(jnp.sum(centred0 * centred0, axis=(0, 1)), ("dp", "tensor")) / everyone
    centred = conv_out - average
    inverse = lax.rsqrt(variance + epsilon)
    normed = centred * inverse
    affine = norm_scale * normed + norm_shift
    sig_affine = jax.nn.sigmoid(affine)
    activated = (affine * sig_affine).astype(jnp.bfloat16)
    conv_output = jnp.einsum(
        "btc,cd->btd", activated, full_weight, preferred_element_type=jnp.float32
    ).astype(jnp.bfloat16)
    grad_act = jnp.einsum("btd,cd->btc", out_grad, full_weight, preferred_element_type=jnp.float32)
    grad_affine = grad_act * (sig_affine + affine * sig_affine * (1.0 - sig_affine))
    sums = all_sum(
        jnp.stack([jnp.sum(grad_affine, axis=(0, 1)), jnp.sum(grad_affine * normed, axis=(0, 1))]),
        ("dp", "tensor"),
    )
    shift_grad, scale_grad = sums[0], sums[1]
    grad_conv = (
        norm_scale
        * inverse
        * (grad_affine - shift_grad / everyone - normed * scale_grad / everyone)
    ).astype(jnp.bfloat16)
    grad_pad = extended(grad_conv, (("tensor", 1),), radius)
    grad_gated = jnp.zeros(gated.shape, jnp.float32)
    for offset in range(taps):
        begin = 2 * radius - offset
        grad_gated = grad_gated + depth_kernel[offset] * grad_pad[:, begin : begin + frames, :]
    grad_wide = grad_conv.astype(jnp.float32)
    kernel_terms = jnp.stack(
        [
            jnp.sum(
                padded[:, offset : offset + frames, :].astype(jnp.float32) * grad_wide, axis=(0, 1)
            )
            for offset in range(taps)
        ]
    )
    kernel_grad = all_sum(kernel_terms, ("dp", "tensor"))
    input_grad = jnp.concatenate(
        [grad_gated * gates, grad_gated * values * gates * (1.0 - gates)], axis=-1
    ).astype(jnp.bfloat16)
    flat_act = activated.reshape(-1, width)
    flat_grad = out_grad.reshape(-1, width)
    act_parts = [lax.dynamic_slice_in_dim(flat_act, me * rows, rows, axis=1)]
    grad_parts = [flat_grad]
    for shift in range(1, peers):
        owner = lax.rem(me + shift, peers)
        block = lax.dynamic_slice_in_dim(flat_act, owner * rows, rows, axis=1)
        act_parts.append(shifted(block, "tensor", shift))
        grad_parts.append(shifted(flat_grad, "tensor", shift))
    local_grad = jnp.einsum(
        "fc,fd->cd",
        jnp.concatenate(act_parts, axis=0),
        jnp.concatenate(grad_parts, axis=0),
        preferred_element_type=jnp.float32,
    )
    weight_grad = lax.psum(local_grad, "dp")
    return (conv_output, input_grad, weight_grad, kernel_grad, scale_grad, shift_grad)


def solution(mesh):
    in_specs = (P("dp", "tensor", None), P(), P(), P(), P("tensor", None), P("dp", "tensor", None))
    out_specs = (P("dp", "tensor", None), P("dp", "tensor", None), P("tensor", None), P(), P(), P())
    return jax.shard_map(
        on_device, mesh=mesh, in_specs=in_specs, out_specs=out_specs, check_vma=False
    )
```

```python
import jax
import jax.numpy as jnp
from jax import lax
from jax.sharding import PartitionSpec as P

epsilon = 1e-05


def extended(array, sides, width):
    for axis, dim in sides:
        peers, length = (lax.axis_size(axis), array.shape[dim])
        up = [(i, (i + 1) % peers) for i in range(peers - 1)]
        down = [(j, i) for i, j in up]
        last = lax.slice_in_dim(array, length - width, length, axis=dim)
        leading = lax.slice_in_dim(array, 0, width, axis=dim)
        before = lax.ppermute(last, axis, up)
        after = lax.ppermute(leading, axis, down)
        array = jnp.concatenate([before, array, after], axis=dim)
    return array


def is_power_of_two(n):
    return n > 0 and (n & (n - 1)) == 0


def all_sum(x, axes):
    for axis in axes:
        peers = lax.axis_size(axis)
        if not is_power_of_two(peers):
            x = lax.psum(x, axis)
            continue
        step = 1
        while step < peers:
            x = x + lax.ppermute(x, axis, [(i, i ^ step) for i in range(peers)])
            step *= 2
    return x


def all_moments(mean, spread, count, axes):
    for axis in axes:
        peers = lax.axis_size(axis)
        step = 1
        while step < peers:
            other = lax.ppermute(jnp.stack([mean, spread]), axis, [(i, i ^ step) for i in range(peers)])
            delta = other[0] - mean
            mean = (mean + other[0]) * 0.5
            spread = (spread + other[1]) + delta * delta * (count * 0.5)
            count = count * 2
            step *= 2
    return mean, spread


def gather_weight(block):
    peers = lax.axis_size("tensor")
    me = lax.axis_index("tensor")
    pairs = lax.axis_size("dp") % 2 == 0
    if pairs:
        half = block.shape[0] // 2
        core = lax.rem(lax.axis_index("dp"), 2)
        mine = lax.dynamic_slice_in_dim(block, core * half, half, axis=0)
    else:
        mine = block
    right = [(i, i + 1) for i in range(peers - 1)]
    left = [(i + 1, i) for i in range(peers - 1)]
    index = lax.broadcasted_iota(jnp.int32, (peers, 1, 1), 0)
    held = jnp.where(index == me, mine[None], jnp.zeros_like(mine)[None])
    going_right, going_left = mine, mine
    for hop in range(1, peers):
        going_right = lax.ppermute(going_right, "tensor", right)
        going_left = lax.ppermute(going_left, "tensor", left)
        held = jnp.where(index == me - hop, going_right[None], held)
        held = jnp.where(index == me + hop, going_left[None], held)
    if pairs:
        other = lax.ppermute(held, "dp", [(i, i ^ 1) for i in range(lax.axis_size("dp"))])
        first = jnp.where(core == 0, held, other)
        second = jnp.where(core == 0, other, held)
        held = jnp.concatenate([first, second], axis=1)
    return held.reshape(peers * block.shape[0], block.shape[1])


def on_device(glu_input, depth_kernel, norm_scale, norm_shift, proj_weight, out_grad):
    width = proj_weight.shape[1]
    rows = proj_weight.shape[0]
    frames = glu_input.shape[1]
    taps = depth_kernel.shape[0]
    radius = (taps - 1) // 2
    peers = lax.axis_size("tensor")
    me = lax.axis_index("tensor")
    local = glu_input.shape[0] * frames
    everyone = local * lax.axis_size("dp") * peers
    full_weight = gather_weight(proj_weight)
    values = glu_input[..., :width].astype(jnp.float32)
    gates = jax.nn.sigmoid(glu_input[..., width:].astype(jnp.float32))
    gated = (values * gates).astype(jnp.bfloat16)
    padded = extended(gated, (("tensor", 1),), radius)
    conv_out = jnp.zeros(gated.shape, jnp.float32)
    for offset in range(taps):
        conv_out = conv_out + depth_kernel[offset] * padded[:, offset : offset + frames, :]
    mean_local = jnp.sum(conv_out, axis=(0, 1)) / local
    dev_local = conv_out - mean_local
    spread_local = jnp.sum(dev_local * dev_local, axis=(0, 1))
    if all(is_power_of_two(lax.axis_size(a)) for a in ("dp", "tensor")):
        average, spread = all_moments(mean_local, spread_local, float(local), ("dp", "tensor"))
        variance = spread / everyone
    else:
        average = lax.psum(jnp.sum(conv_out, axis=(0, 1)), ("dp", "tensor")) / everyone
        centred0 = conv_out - average
        variance = lax.psum(jnp.sum(centred0 * centred0, axis=(0, 1)), ("dp", "tensor")) / everyone
    centred = conv_out - average
    inverse = lax.rsqrt(variance + epsilon)
    normed = centred * inverse
    affine = norm_scale * normed + norm_shift
    sig_affine = jax.nn.sigmoid(affine)
    activated = (affine * sig_affine).astype(jnp.bfloat16)
    conv_output = jnp.einsum(
        "btc,cd->btd", activated, full_weight, preferred_element_type=jnp.float32
    ).astype(jnp.bfloat16)
    grad_act = jnp.einsum("btd,cd->btc", out_grad, full_weight, preferred_element_type=jnp.float32)
    grad_affine = grad_act * (sig_affine + affine * sig_affine * (1.0 - sig_affine))
    sums = all_sum(
        jnp.stack([jnp.sum(grad_affine, axis=(0, 1)), jnp.sum(grad_affine * normed, axis=(0, 1))]),
        ("dp", "tensor"),
    )
    shift_grad, scale_grad = sums[0], sums[1]
    grad_conv = (
        norm_scale
        * inverse
        * (grad_affine - shift_grad / everyone - normed * scale_grad / everyone)
    ).astype(jnp.bfloat16)
    grad_pad = extended(grad_conv, (("tensor", 1),), radius)
    grad_gated = jnp.zeros(gated.shape, jnp.float32)
    for offset in range(taps):
        begin = 2 * radius - offset
        grad_gated = grad_gated + depth_kernel[offset] * grad_pad[:, begin : begin + frames, :]
    grad_wide = grad_conv.astype(jnp.float32)
    kernel_terms = jnp.stack(
        [
            jnp.sum(
                padded[:, offset : offset + frames, :].astype(jnp.float32) * grad_wide, axis=(0, 1)
            )
            for offset in range(taps)
        ]
    )
    kernel_grad = all_sum(kernel_terms, ("dp", "tensor"))
    input_grad = jnp.concatenate(
        [grad_gated * gates, grad_gated * values * gates * (1.0 - gates)], axis=-1
    ).astype(jnp.bfloat16)
    flat_act = activated.reshape(-1, width)
    flat_grad = out_grad.reshape(-1, width)
    group_grad = lax.all_gather(flat_grad, "tensor", axis=0, tiled=True)
    group_act = lax.all_to_all(flat_act, "tensor", split_axis=1, concat_axis=0, tiled=True)
    local_grad = jnp.einsum("fc,fd->cd", group_act, group_grad, preferred_element_type=jnp.float32)
    weight_grad = lax.psum(local_grad, "dp")
    return (conv_output, input_grad, weight_grad, kernel_grad, scale_grad, shift_grad)


def solution(mesh):
    in_specs = (P("dp", "tensor", None), P(), P(), P(), P("tensor", None), P("dp", "tensor", None))
    out_specs = (P("dp", "tensor", None), P("dp", "tensor", None), P("tensor", None), P(), P(), P())
    return jax.shard_map(
        on_device, mesh=mesh, in_specs=in_specs, out_specs=out_specs, check_vma=False
    )
```

```python
import jax
import jax.numpy as jnp
from jax import lax
from jax.sharding import PartitionSpec as P

epsilon = 1e-05


def extended(array, sides, width):
    for axis, dim in sides:
        peers, length = (lax.axis_size(axis), array.shape[dim])
        up = [(i, (i + 1) % peers) for i in range(peers - 1)]
        down = [(j, i) for i, j in up]
        last = lax.slice_in_dim(array, length - width, length, axis=dim)
        leading = lax.slice_in_dim(array, 0, width, axis=dim)
        before = lax.ppermute(last, axis, up)
        after = lax.ppermute(leading, axis, down)
        array = jnp.concatenate([before, array, after], axis=dim)
    return array


def is_power_of_two(n):
    return n > 0 and (n & (n - 1)) == 0


def all_sum(x, axes):
    for axis in axes:
        peers = lax.axis_size(axis)
        if not is_power_of_two(peers):
            x = lax.psum(x, axis)
            continue
        step = 1
        while step < peers:
            x = x + lax.ppermute(x, axis, [(i, i ^ step) for i in range(peers)])
            step *= 2
    return x


def all_moments(mean, spread, count, axes):
    for axis in axes:
        peers = lax.axis_size(axis)
        step = 1
        while step < peers:
            other = lax.ppermute(jnp.stack([mean, spread]), axis, [(i, i ^ step) for i in range(peers)])
            delta = other[0] - mean
            mean = (mean + other[0]) * 0.5
            spread = (spread + other[1]) + delta * delta * (count * 0.5)
            count = count * 2
            step *= 2
    return mean, spread


def rows_sum(x, axis):
    peers = lax.axis_size(axis)
    if not is_power_of_two(peers) or x.shape[0] % peers:
        return lax.psum(x, axis)
    me = lax.axis_index(axis)
    bits = []
    step = 1
    while step < peers:
        bit = lax.rem(me // step, 2)
        half = x.shape[0] // 2
        keep = lax.dynamic_slice_in_dim(x, bit * half, half, axis=0)
        give = lax.dynamic_slice_in_dim(x, (1 - bit) * half, half, axis=0)
        x = keep + lax.ppermute(give, axis, [(i, i ^ step) for i in range(peers)])
        bits.append((step, bit))
        step *= 2
    for step, bit in reversed(bits):
        other = lax.ppermute(x, axis, [(i, i ^ step) for i in range(peers)])
        x = jnp.where(bit == 0, jnp.concatenate([x, other]), jnp.concatenate([other, x]))
    return x


def gather_weight(block):
    peers = lax.axis_size("tensor")
    me = lax.axis_index("tensor")
    pairs = lax.axis_size("dp") % 2 == 0
    if pairs:
        half = block.shape[0] // 2
        core = lax.rem(lax.axis_index("dp"), 2)
        mine = lax.dynamic_slice_in_dim(block, core * half, half, axis=0)
    else:
        mine = block
    right = [(i, i + 1) for i in range(peers - 1)]
    left = [(i + 1, i) for i in range(peers - 1)]
    index = lax.broadcasted_iota(jnp.int32, (peers, 1, 1), 0)
    held = jnp.where(index == me, mine[None], jnp.zeros_like(mine)[None])
    going_right, going_left = mine, mine
    for hop in range(1, peers):
        going_right = lax.ppermute(going_right, "tensor", right)
        going_left = lax.ppermute(going_left, "tensor", left)
        held = jnp.where(index == me - hop, going_right[None], held)
        held = jnp.where(index == me + hop, going_left[None], held)
    if pairs:
        other = lax.ppermute(held, "dp", [(i, i ^ 1) for i in range(lax.axis_size("dp"))])
        first = jnp.where(core == 0, held, other)
        second = jnp.where(core == 0, other, held)
        held = jnp.concatenate([first, second], axis=1)
    return held.reshape(peers * block.shape[0], block.shape[1])


def on_device(glu_input, depth_kernel, norm_scale, norm_shift, proj_weight, out_grad):
    width = proj_weight.shape[1]
    rows = proj_weight.shape[0]
    frames = glu_input.shape[1]
    taps = depth_kernel.shape[0]
    radius = (taps - 1) // 2
    peers = lax.axis_size("tensor")
    me = lax.axis_index("tensor")
    local = glu_input.shape[0] * frames
    everyone = local * lax.axis_size("dp") * peers
    full_weight = gather_weight(proj_weight)
    flat_grad = out_grad.reshape(-1, width)
    group_grad = lax.all_gather(flat_grad, "tensor", axis=0, tiled=True)
    values = glu_input[..., :width].astype(jnp.float32)
    gates = jax.nn.sigmoid(glu_input[..., width:].astype(jnp.float32))
    gated = (values * gates).astype(jnp.bfloat16)
    padded = extended(gated, (("tensor", 1),), radius)
    conv_out = jnp.zeros(gated.shape, jnp.float32)
    for offset in range(taps):
        conv_out = conv_out + depth_kernel[offset] * padded[:, offset : offset + frames, :]
    mean_local = jnp.sum(conv_out, axis=(0, 1)) / local
    dev_local = conv_out - mean_local
    spread_local = jnp.sum(dev_local * dev_local, axis=(0, 1))
    if all(is_power_of_two(lax.axis_size(a)) for a in ("dp", "tensor")):
        average, spread = all_moments(mean_local, spread_local, float(local), ("dp", "tensor"))
        variance = spread / everyone
    else:
        average = lax.psum(jnp.sum(conv_out, axis=(0, 1)), ("dp", "tensor")) / everyone
        centred0 = conv_out - average
        variance = lax.psum(jnp.sum(centred0 * centred0, axis=(0, 1)), ("dp", "tensor")) / everyone
    centred = conv_out - average
    inverse = lax.rsqrt(variance + epsilon)
    normed = centred * inverse
    affine = norm_scale * normed + norm_shift
    sig_affine = jax.nn.sigmoid(affine)
    activated = (affine * sig_affine).astype(jnp.bfloat16)
    full_weight, group_grad = lax.optimization_barrier((full_weight, group_grad))
    flat_act = activated.reshape(-1, width)
    group_act = lax.all_to_all(flat_act, "tensor", split_axis=1, concat_axis=0, tiled=True)
    local_grad = jnp.einsum("fc,fd->cd", group_act, group_grad, preferred_element_type=jnp.float32)
    conv_output = jnp.einsum(
        "btc,cd->btd", activated, full_weight, preferred_element_type=jnp.float32
    ).astype(jnp.bfloat16)
    grad_act = jnp.einsum("btd,cd->btc", out_grad, full_weight, preferred_element_type=jnp.float32)
    grad_affine = grad_act * (sig_affine + affine * sig_affine * (1.0 - sig_affine))
    sums = jnp.stack([jnp.sum(grad_affine, axis=(0, 1)), jnp.sum(grad_affine * normed, axis=(0, 1))])
    local_grad, sums = lax.optimization_barrier((local_grad, sums))
    weight_grad = rows_sum(local_grad, "dp")
    sums = all_sum(sums, ("dp", "tensor"))
    shift_grad, scale_grad = sums[0], sums[1]
    grad_conv = (
        norm_scale
        * inverse
        * (grad_affine - shift_grad / everyone - normed * scale_grad / everyone)
    ).astype(jnp.bfloat16)
    grad_pad = extended(grad_conv, (("tensor", 1),), radius)
    grad_gated = jnp.zeros(gated.shape, jnp.float32)
    for offset in range(taps):
        begin = 2 * radius - offset
        grad_gated = grad_gated + depth_kernel[offset] * grad_pad[:, begin : begin + frames, :]
    grad_wide = grad_conv.astype(jnp.float32)
    kernel_terms = jnp.stack(
        [
            jnp.sum(
                padded[:, offset : offset + frames, :].astype(jnp.float32) * grad_wide, axis=(0, 1)
            )
            for offset in range(taps)
        ]
    )
    kernel_grad = all_sum(kernel_terms, ("dp", "tensor"))
    input_grad = jnp.concatenate(
        [grad_gated * gates, grad_gated * values * gates * (1.0 - gates)], axis=-1
    ).astype(jnp.bfloat16)
    return (conv_output, input_grad, weight_grad, kernel_grad, scale_grad, shift_grad)


def solution(mesh):
    in_specs = (P("dp", "tensor", None), P(), P(), P(), P("tensor", None), P("dp", "tensor", None))
    out_specs = (P("dp", "tensor", None), P("dp", "tensor", None), P("tensor", None), P(), P(), P())
    return jax.shard_map(
        on_device, mesh=mesh, in_specs=in_specs, out_specs=out_specs, check_vma=False
    )
```

```python
import jax
import jax.numpy as jnp
from jax import lax
from jax.sharding import PartitionSpec as P

epsilon = 1e-05


def extended(array, sides, width):
    for axis, dim in sides:
        peers, length = (lax.axis_size(axis), array.shape[dim])
        up = [(i, (i + 1) % peers) for i in range(peers - 1)]
        down = [(j, i) for i, j in up]
        last = lax.slice_in_dim(array, length - width, length, axis=dim)
        leading = lax.slice_in_dim(array, 0, width, axis=dim)
        before = lax.ppermute(last, axis, up)
        after = lax.ppermute(leading, axis, down)
        array = jnp.concatenate([before, array, after], axis=dim)
    return array


def is_power_of_two(n):
    return n > 0 and (n & (n - 1)) == 0


def all_sum(x, axes):
    for axis in axes:
        peers = lax.axis_size(axis)
        if not is_power_of_two(peers):
            x = lax.psum(x, axis)
            continue
        step = 1
        while step < peers:
            x = x + lax.ppermute(x, axis, [(i, i ^ step) for i in range(peers)])
            step *= 2
    return x


def all_moments(mean, spread, count, axes):
    for axis in axes:
        peers = lax.axis_size(axis)
        step = 1
        while step < peers:
            other = lax.ppermute(jnp.stack([mean, spread]), axis, [(i, i ^ step) for i in range(peers)])
            delta = other[0] - mean
            mean = (mean + other[0]) * 0.5
            spread = (spread + other[1]) + delta * delta * (count * 0.5)
            count = count * 2
            step *= 2
    return mean, spread


def rows_sum(x, axis):
    peers = lax.axis_size(axis)
    if not is_power_of_two(peers) or x.shape[0] % peers:
        return lax.psum(x, axis)
    me = lax.axis_index(axis)
    bits = []
    step = 1
    while step < peers:
        bit = lax.rem(me // step, 2)
        half = x.shape[0] // 2
        keep = lax.dynamic_slice_in_dim(x, bit * half, half, axis=0)
        give = lax.dynamic_slice_in_dim(x, (1 - bit) * half, half, axis=0)
        x = keep + lax.ppermute(give, axis, [(i, i ^ step) for i in range(peers)])
        bits.append((step, bit))
        step *= 2
    for step, bit in reversed(bits):
        other = lax.ppermute(x, axis, [(i, i ^ step) for i in range(peers)])
        x = jnp.where(bit == 0, jnp.concatenate([x, other]), jnp.concatenate([other, x]))
    return x


def gather_weight(block):
    if lax.axis_size("dp") % 2:
        return lax.all_gather(block, "tensor", axis=0, tiled=True)
    peers = lax.axis_size("tensor")
    half = block.shape[0] // 2
    core = lax.rem(lax.axis_index("dp"), 2)
    mine = lax.dynamic_slice_in_dim(block, core * half, half, axis=0)
    held = lax.all_gather(mine, "tensor", axis=0, tiled=False)
    other = lax.ppermute(held, "dp", [(i, i ^ 1) for i in range(lax.axis_size("dp"))])
    first = jnp.where(core == 0, held, other)
    second = jnp.where(core == 0, other, held)
    return jnp.concatenate([first, second], axis=1).reshape(peers * block.shape[0], block.shape[1])


def on_device(glu_input, depth_kernel, norm_scale, norm_shift, proj_weight, out_grad):
    width = proj_weight.shape[1]
    rows = proj_weight.shape[0]
    frames = glu_input.shape[1]
    taps = depth_kernel.shape[0]
    radius = (taps - 1) // 2
    peers = lax.axis_size("tensor")
    me = lax.axis_index("tensor")
    local = glu_input.shape[0] * frames
    everyone = local * lax.axis_size("dp") * peers
    full_weight = gather_weight(proj_weight)
    flat_grad = out_grad.reshape(-1, width)
    group_grad = lax.all_gather(flat_grad, "tensor", axis=0, tiled=True)
    values = glu_input[..., :width].astype(jnp.float32)
    gates = jax.nn.sigmoid(glu_input[..., width:].astype(jnp.float32))
    gated = (values * gates).astype(jnp.bfloat16)
    padded = extended(gated, (("tensor", 1),), radius)
    conv_out = jnp.zeros(gated.shape, jnp.float32)
    for offset in range(taps):
        conv_out = conv_out + depth_kernel[offset] * padded[:, offset : offset + frames, :]
    mean_local = jnp.sum(conv_out, axis=(0, 1)) / local
    dev_local = conv_out - mean_local
    spread_local = jnp.sum(dev_local * dev_local, axis=(0, 1))
    if all(is_power_of_two(lax.axis_size(a)) for a in ("dp", "tensor")):
        average, spread = all_moments(mean_local, spread_local, float(local), ("dp", "tensor"))
        variance = spread / everyone
    else:
        average = lax.psum(jnp.sum(conv_out, axis=(0, 1)), ("dp", "tensor")) / everyone
        centred0 = conv_out - average
        variance = lax.psum(jnp.sum(centred0 * centred0, axis=(0, 1)), ("dp", "tensor")) / everyone
    centred = conv_out - average
    inverse = lax.rsqrt(variance + epsilon)
    normed = centred * inverse
    affine = norm_scale * normed + norm_shift
    sig_affine = jax.nn.sigmoid(affine)
    activated = (affine * sig_affine).astype(jnp.bfloat16)
    flat_act = activated.reshape(-1, width)
    group_act = lax.all_to_all(flat_act, "tensor", split_axis=1, concat_axis=0, tiled=True)
    local_grad = jnp.einsum("fc,fd->cd", group_act, group_grad, preferred_element_type=jnp.float32)
    conv_output = jnp.einsum(
        "btc,cd->btd", activated, full_weight, preferred_element_type=jnp.float32
    ).astype(jnp.bfloat16)
    grad_act = jnp.einsum("btd,cd->btc", out_grad, full_weight, preferred_element_type=jnp.float32)
    grad_affine = grad_act * (sig_affine + affine * sig_affine * (1.0 - sig_affine))
    sums = jnp.stack([jnp.sum(grad_affine, axis=(0, 1)), jnp.sum(grad_affine * normed, axis=(0, 1))])
    sums = all_sum(sums, ("dp", "tensor"))
    shift_grad, scale_grad = sums[0], sums[1]
    grad_conv = (
        norm_scale
        * inverse
        * (grad_affine - shift_grad / everyone - normed * scale_grad / everyone)
    ).astype(jnp.bfloat16)
    grad_pad = extended(grad_conv, (("tensor", 1),), radius)
    grad_gated = jnp.zeros(gated.shape, jnp.float32)
    for offset in range(taps):
        begin = 2 * radius - offset
        grad_gated = grad_gated + depth_kernel[offset] * grad_pad[:, begin : begin + frames, :]
    grad_wide = grad_conv.astype(jnp.float32)
    kernel_terms = jnp.stack(
        [
            jnp.sum(
                padded[:, offset : offset + frames, :].astype(jnp.float32) * grad_wide, axis=(0, 1)
            )
            for offset in range(taps)
        ]
    )
    local_grad, kernel_terms = lax.optimization_barrier((local_grad, kernel_terms))
    weight_grad = rows_sum(local_grad, "dp")
    kernel_grad = all_sum(kernel_terms, ("dp", "tensor"))
    input_grad = jnp.concatenate(
        [grad_gated * gates, grad_gated * values * gates * (1.0 - gates)], axis=-1
    ).astype(jnp.bfloat16)
    return (conv_output, input_grad, weight_grad, kernel_grad, scale_grad, shift_grad)


def solution(mesh):
    in_specs = (P("dp", "tensor", None), P(), P(), P(), P("tensor", None), P("dp", "tensor", None))
    out_specs = (P("dp", "tensor", None), P("dp", "tensor", None), P("tensor", None), P(), P(), P())
    return jax.shard_map(
        on_device, mesh=mesh, in_specs=in_specs, out_specs=out_specs, check_vma=False
    )
```

```python
import jax
import jax.numpy as jnp
from jax import lax
from jax.sharding import PartitionSpec as P

epsilon = 1e-05


def extended(array, sides, width):
    for axis, dim in sides:
        peers, length = (lax.axis_size(axis), array.shape[dim])
        up = [(i, (i + 1) % peers) for i in range(peers - 1)]
        down = [(j, i) for i, j in up]
        last = lax.slice_in_dim(array, length - width, length, axis=dim)
        leading = lax.slice_in_dim(array, 0, width, axis=dim)
        before = lax.ppermute(last, axis, up)
        after = lax.ppermute(leading, axis, down)
        array = jnp.concatenate([before, array, after], axis=dim)
    return array


def is_power_of_two(n):
    return n > 0 and (n & (n - 1)) == 0


def all_sum(x, axes):
    for axis in axes:
        peers = lax.axis_size(axis)
        if not is_power_of_two(peers):
            x = lax.psum(x, axis)
            continue
        step = 1
        while step < peers:
            x = x + lax.ppermute(x, axis, [(i, i ^ step) for i in range(peers)])
            step *= 2
    return x


def all_moments(mean, spread, count, axes):
    for axis in axes:
        peers = lax.axis_size(axis)
        step = 1
        while step < peers:
            other = lax.ppermute(jnp.stack([mean, spread]), axis, [(i, i ^ step) for i in range(peers)])
            delta = other[0] - mean
            mean = (mean + other[0]) * 0.5
            spread = (spread + other[1]) + delta * delta * (count * 0.5)
            count = count * 2
            step *= 2
    return mean, spread


def rows_sum(x, axis):
    peers = lax.axis_size(axis)
    if not is_power_of_two(peers) or x.shape[0] % peers:
        return lax.psum(x, axis)
    me = lax.axis_index(axis)
    bits = []
    step = 1
    while step < peers:
        bit = lax.rem(me // step, 2)
        half = x.shape[0] // 2
        keep = lax.dynamic_slice_in_dim(x, bit * half, half, axis=0)
        give = lax.dynamic_slice_in_dim(x, (1 - bit) * half, half, axis=0)
        x = keep + lax.ppermute(give, axis, [(i, i ^ step) for i in range(peers)])
        bits.append((step, bit))
        step *= 2
    for step, bit in reversed(bits):
        other = lax.ppermute(x, axis, [(i, i ^ step) for i in range(peers)])
        x = jnp.where(bit == 0, jnp.concatenate([x, other]), jnp.concatenate([other, x]))
    return x


def gather_weight(block):
    if lax.axis_size("dp") % 2:
        return lax.all_gather(block, "tensor", axis=0, tiled=True)
    peers = lax.axis_size("tensor")
    half = block.shape[0] // 2
    core = lax.rem(lax.axis_index("dp"), 2)
    mine = lax.dynamic_slice_in_dim(block, core * half, half, axis=0)
    held = lax.all_gather(mine, "tensor", axis=0, tiled=False)
    other = lax.ppermute(held, "dp", [(i, i ^ 1) for i in range(lax.axis_size("dp"))])
    first = jnp.where(core == 0, held, other)
    second = jnp.where(core == 0, other, held)
    return jnp.concatenate([first, second], axis=1).reshape(peers * block.shape[0], block.shape[1])


def on_device(glu_input, depth_kernel, norm_scale, norm_shift, proj_weight, out_grad):
    width = proj_weight.shape[1]
    rows = proj_weight.shape[0]
    frames = glu_input.shape[1]
    taps = depth_kernel.shape[0]
    radius = (taps - 1) // 2
    peers = lax.axis_size("tensor")
    me = lax.axis_index("tensor")
    local = glu_input.shape[0] * frames
    everyone = local * lax.axis_size("dp") * peers
    flat_grad = out_grad.reshape(-1, width)
    group_grad = lax.all_gather(flat_grad, "tensor", axis=0, tiled=True)
    own_columns = jnp.einsum("fd,cd->fc", group_grad, proj_weight, preferred_element_type=jnp.float32)
    grad_act = lax.all_to_all(own_columns, "tensor", split_axis=0, concat_axis=1, tiled=True)
    grad_act = grad_act.reshape(out_grad.shape)
    values = glu_input[..., :width].astype(jnp.float32)
    gates = jax.nn.sigmoid(glu_input[..., width:].astype(jnp.float32))
    gated = (values * gates).astype(jnp.bfloat16)
    padded = extended(gated, (("tensor", 1),), radius)
    conv_out = jnp.zeros(gated.shape, jnp.float32)
    for offset in range(taps):
        conv_out = conv_out + depth_kernel[offset] * padded[:, offset : offset + frames, :]
    mean_local = jnp.sum(conv_out, axis=(0, 1)) / local
    dev_local = conv_out - mean_local
    spread_local = jnp.sum(dev_local * dev_local, axis=(0, 1))
    if all(is_power_of_two(lax.axis_size(a)) for a in ("dp", "tensor")):
        average, spread = all_moments(mean_local, spread_local, float(local), ("dp", "tensor"))
        variance = spread / everyone
    else:
        average = lax.psum(jnp.sum(conv_out, axis=(0, 1)), ("dp", "tensor")) / everyone
        centred0 = conv_out - average
        variance = lax.psum(jnp.sum(centred0 * centred0, axis=(0, 1)), ("dp", "tensor")) / everyone
    centred = conv_out - average
    inverse = lax.rsqrt(variance + epsilon)
    normed = centred * inverse
    affine = norm_scale * normed + norm_shift
    sig_affine = jax.nn.sigmoid(affine)
    activated = (affine * sig_affine).astype(jnp.bfloat16)
    flat_act = activated.reshape(-1, width)
    group_act = lax.all_to_all(flat_act, "tensor", split_axis=1, concat_axis=0, tiled=True)
    local_grad = jnp.einsum("fc,fd->cd", group_act, group_grad, preferred_element_type=jnp.float32)
    grad_affine = grad_act * (sig_affine + affine * sig_affine * (1.0 - sig_affine))
    sums = jnp.stack([jnp.sum(grad_affine, axis=(0, 1)), jnp.sum(grad_affine * normed, axis=(0, 1))])
    sums = all_sum(sums, ("dp", "tensor"))
    shift_grad, scale_grad = sums[0], sums[1]
    grad_conv = (
        norm_scale
        * inverse
        * (grad_affine - shift_grad / everyone - normed * scale_grad / everyone)
    ).astype(jnp.bfloat16)
    grad_pad = extended(grad_conv, (("tensor", 1),), radius)
    grad_gated = jnp.zeros(gated.shape, jnp.float32)
    for offset in range(taps):
        begin = 2 * radius - offset
        grad_gated = grad_gated + depth_kernel[offset] * grad_pad[:, begin : begin + frames, :]
    grad_wide = grad_conv.astype(jnp.float32)
    kernel_terms = jnp.stack(
        [
            jnp.sum(
                padded[:, offset : offset + frames, :].astype(jnp.float32) * grad_wide, axis=(0, 1)
            )
            for offset in range(taps)
        ]
    )
    local_grad, kernel_terms = lax.optimization_barrier((local_grad, kernel_terms))
    weight_grad = rows_sum(local_grad, "dp")
    kernel_grad = all_sum(kernel_terms, ("dp", "tensor"))
    input_grad = jnp.concatenate(
        [grad_gated * gates, grad_gated * values * gates * (1.0 - gates)], axis=-1
    ).astype(jnp.bfloat16)
    full_weight = gather_weight(proj_weight)
    conv_output = jnp.einsum(
        "btc,cd->btd", activated, full_weight, preferred_element_type=jnp.float32
    ).astype(jnp.bfloat16)
    return (conv_output, input_grad, weight_grad, kernel_grad, scale_grad, shift_grad)


def solution(mesh):
    in_specs = (P("dp", "tensor", None), P(), P(), P(), P("tensor", None), P("dp", "tensor", None))
    out_specs = (P("dp", "tensor", None), P("dp", "tensor", None), P("tensor", None), P(), P(), P())
    return jax.shard_map(
        on_device, mesh=mesh, in_specs=in_specs, out_specs=out_specs, check_vma=False
    )
```

```python
import jax
import jax.numpy as jnp
from jax import lax
from jax.sharding import PartitionSpec as P

epsilon = 1e-05


def extended(array, sides, width):
    for axis, dim in sides:
        peers, length = (lax.axis_size(axis), array.shape[dim])
        up = [(i, (i + 1) % peers) for i in range(peers - 1)]
        down = [(j, i) for i, j in up]
        last = lax.slice_in_dim(array, length - width, length, axis=dim)
        leading = lax.slice_in_dim(array, 0, width, axis=dim)
        before = lax.ppermute(last, axis, up)
        after = lax.ppermute(leading, axis, down)
        array = jnp.concatenate([before, array, after], axis=dim)
    return array


def is_power_of_two(n):
    return n > 0 and (n & (n - 1)) == 0


def all_sum(x, axes):
    for axis in axes:
        peers = lax.axis_size(axis)
        if not is_power_of_two(peers):
            x = lax.psum(x, axis)
            continue
        step = 1
        while step < peers:
            x = x + lax.ppermute(x, axis, [(i, i ^ step) for i in range(peers)])
            step *= 2
    return x


def all_moments(mean, spread, count, axes):
    for axis in axes:
        peers = lax.axis_size(axis)
        step = 1
        while step < peers:
            other = lax.ppermute(jnp.stack([mean, spread]), axis, [(i, i ^ step) for i in range(peers)])
            delta = other[0] - mean
            mean = (mean + other[0]) * 0.5
            spread = (spread + other[1]) + delta * delta * (count * 0.5)
            count = count * 2
            step *= 2
    return mean, spread


def rows_sum(x, axis):
    peers = lax.axis_size(axis)
    if not is_power_of_two(peers) or x.shape[0] % peers:
        return lax.psum(x, axis)
    me = lax.axis_index(axis)
    bits = []
    step = 1
    while step < peers:
        bit = lax.rem(me // step, 2)
        half = x.shape[0] // 2
        keep = lax.dynamic_slice_in_dim(x, bit * half, half, axis=0)
        give = lax.dynamic_slice_in_dim(x, (1 - bit) * half, half, axis=0)
        x = keep + lax.ppermute(give, axis, [(i, i ^ step) for i in range(peers)])
        bits.append((step, bit))
        step *= 2
    for step, bit in reversed(bits):
        other = lax.ppermute(x, axis, [(i, i ^ step) for i in range(peers)])
        x = jnp.where(bit == 0, jnp.concatenate([x, other]), jnp.concatenate([other, x]))
    return x


def gather_weight(block):
    if lax.axis_size("dp") % 2:
        return lax.all_gather(block, "tensor", axis=0, tiled=True)
    peers = lax.axis_size("tensor")
    half = block.shape[0] // 2
    core = lax.rem(lax.axis_index("dp"), 2)
    mine = lax.dynamic_slice_in_dim(block, core * half, half, axis=0)
    held = lax.all_gather(mine, "tensor", axis=0, tiled=False)
    other = lax.ppermute(held, "dp", [(i, i ^ 1) for i in range(lax.axis_size("dp"))])
    first = jnp.where(core == 0, held, other)
    second = jnp.where(core == 0, other, held)
    return jnp.concatenate([first, second], axis=1).reshape(peers * block.shape[0], block.shape[1])


def on_device(glu_input, depth_kernel, norm_scale, norm_shift, proj_weight, out_grad):
    width = proj_weight.shape[1]
    rows = proj_weight.shape[0]
    frames = glu_input.shape[1]
    taps = depth_kernel.shape[0]
    radius = (taps - 1) // 2
    peers = lax.axis_size("tensor")
    me = lax.axis_index("tensor")
    local = glu_input.shape[0] * frames
    everyone = local * lax.axis_size("dp") * peers
    flat_grad = out_grad.reshape(-1, width)
    group_grad = lax.all_gather(flat_grad, "tensor", axis=0, tiled=True)
    own_columns = jnp.einsum("fd,cd->fc", group_grad, proj_weight, preferred_element_type=jnp.float32)
    grad_act = lax.all_to_all(own_columns, "tensor", split_axis=0, concat_axis=1, tiled=True)
    grad_act = grad_act.reshape(out_grad.shape)
    values = glu_input[..., :width].astype(jnp.float32)
    gates = jax.nn.sigmoid(glu_input[..., width:].astype(jnp.float32))
    gated = (values * gates).astype(jnp.bfloat16)
    padded = extended(gated, (("tensor", 1),), radius)
    conv_out = jnp.zeros(gated.shape, jnp.float32)
    for offset in range(taps):
        conv_out = conv_out + depth_kernel[offset] * padded[:, offset : offset + frames, :]
    mean_local = jnp.sum(conv_out, axis=(0, 1)) / local
    dev_local = conv_out - mean_local
    spread_local = jnp.sum(dev_local * dev_local, axis=(0, 1))
    if all(is_power_of_two(lax.axis_size(a)) for a in ("dp", "tensor")):
        average, spread = all_moments(mean_local, spread_local, float(local), ("dp", "tensor"))
        variance = spread / everyone
    else:
        average = lax.psum(jnp.sum(conv_out, axis=(0, 1)), ("dp", "tensor")) / everyone
        centred0 = conv_out - average
        variance = lax.psum(jnp.sum(centred0 * centred0, axis=(0, 1)), ("dp", "tensor")) / everyone
    centred = conv_out - average
    inverse = lax.rsqrt(variance + epsilon)
    normed = centred * inverse
    affine = norm_scale * normed + norm_shift
    sig_affine = jax.nn.sigmoid(affine)
    activated = (affine * sig_affine).astype(jnp.bfloat16)
    flat_act = activated.reshape(-1, width)
    group_act = lax.all_to_all(flat_act, "tensor", split_axis=1, concat_axis=0, tiled=True)
    local_grad = jnp.einsum("fc,fd->cd", group_act, group_grad, preferred_element_type=jnp.float32)
    grad_affine = grad_act * (sig_affine + affine * sig_affine * (1.0 - sig_affine))
    sums = jnp.stack([jnp.sum(grad_affine, axis=(0, 1)), jnp.sum(grad_affine * normed, axis=(0, 1))])
    sums = all_sum(sums, ("dp", "tensor"))
    shift_grad, scale_grad = sums[0], sums[1]
    grad_conv = (
        norm_scale
        * inverse
        * (grad_affine - shift_grad / everyone - normed * scale_grad / everyone)
    ).astype(jnp.bfloat16)
    grad_pad = extended(grad_conv, (("tensor", 1),), radius)
    grad_gated = jnp.zeros(gated.shape, jnp.float32)
    for offset in range(taps):
        begin = 2 * radius - offset
        grad_gated = grad_gated + depth_kernel[offset] * grad_pad[:, begin : begin + frames, :]
    grad_wide = grad_conv.astype(jnp.float32)
    kernel_terms = jnp.stack(
        [
            jnp.sum(
                padded[:, offset : offset + frames, :].astype(jnp.float32) * grad_wide, axis=(0, 1)
            )
            for offset in range(taps)
        ]
    )
    full_weight = gather_weight(proj_weight)
    full_weight, local_grad, kernel_terms = lax.optimization_barrier((full_weight, local_grad, kernel_terms))
    weight_grad = rows_sum(local_grad, "dp")
    kernel_grad = all_sum(kernel_terms, ("dp", "tensor"))
    input_grad = jnp.concatenate(
        [grad_gated * gates, grad_gated * values * gates * (1.0 - gates)], axis=-1
    ).astype(jnp.bfloat16)
    conv_output = jnp.einsum(
        "btc,cd->btd", activated, full_weight, preferred_element_type=jnp.float32
    ).astype(jnp.bfloat16)
    return (conv_output, input_grad, weight_grad, kernel_grad, scale_grad, shift_grad)


def solution(mesh):
    in_specs = (P("dp", "tensor", None), P(), P(), P(), P("tensor", None), P("dp", "tensor", None))
    out_specs = (P("dp", "tensor", None), P("dp", "tensor", None), P("tensor", None), P(), P(), P())
    return jax.shard_map(
        on_device, mesh=mesh, in_specs=in_specs, out_specs=out_specs, check_vma=False
    )
```

```python
import jax
import jax.numpy as jnp
from jax import lax
from jax.sharding import PartitionSpec as P

epsilon = 1e-05


def extended(array, sides, width):
    for axis, dim in sides:
        peers, length = (lax.axis_size(axis), array.shape[dim])
        up = [(i, (i + 1) % peers) for i in range(peers - 1)]
        down = [(j, i) for i, j in up]
        last = lax.slice_in_dim(array, length - width, length, axis=dim)
        leading = lax.slice_in_dim(array, 0, width, axis=dim)
        before = lax.ppermute(last, axis, up)
        after = lax.ppermute(leading, axis, down)
        array = jnp.concatenate([before, array, after], axis=dim)
    return array


def is_power_of_two(n):
    return n > 0 and (n & (n - 1)) == 0


def all_sum(x, axes):
    for axis in axes:
        peers = lax.axis_size(axis)
        if not is_power_of_two(peers):
            x = lax.psum(x, axis)
            continue
        step = 1
        while step < peers:
            x = x + lax.ppermute(x, axis, [(i, i ^ step) for i in range(peers)])
            step *= 2
    return x


def all_moments(mean, spread, count, axes):
    for axis in axes:
        peers = lax.axis_size(axis)
        step = 1
        while step < peers:
            other = lax.ppermute(jnp.stack([mean, spread]), axis, [(i, i ^ step) for i in range(peers)])
            delta = other[0] - mean
            mean = (mean + other[0]) * 0.5
            spread = (spread + other[1]) + delta * delta * (count * 0.5)
            count = count * 2
            step *= 2
    return mean, spread


def rows_sum(x, axis):
    peers = lax.axis_size(axis)
    if not is_power_of_two(peers) or x.shape[0] % peers:
        return lax.psum(x, axis)
    me = lax.axis_index(axis)
    bits = []
    step = 1
    while step < peers:
        bit = lax.rem(me // step, 2)
        half = x.shape[0] // 2
        keep = lax.dynamic_slice_in_dim(x, bit * half, half, axis=0)
        give = lax.dynamic_slice_in_dim(x, (1 - bit) * half, half, axis=0)
        x = keep + lax.ppermute(give, axis, [(i, i ^ step) for i in range(peers)])
        bits.append((step, bit))
        step *= 2
    for step, bit in reversed(bits):
        other = lax.ppermute(x, axis, [(i, i ^ step) for i in range(peers)])
        x = jnp.where(bit == 0, jnp.concatenate([x, other]), jnp.concatenate([other, x]))
    return x


def gather_weight(block):
    group = lax.axis_size("dp")
    if block.shape[0] % group:
        return lax.all_gather(block, "tensor", axis=0, tiled=True)
    piece = block.shape[0] // group
    mine = lax.dynamic_slice_in_dim(block, lax.axis_index("dp") * piece, piece, axis=0)
    return lax.all_gather(mine, ("tensor", "dp"), axis=0, tiled=True)


def on_device(glu_input, depth_kernel, norm_scale, norm_shift, proj_weight, out_grad):
    width = proj_weight.shape[1]
    rows = proj_weight.shape[0]
    frames = glu_input.shape[1]
    taps = depth_kernel.shape[0]
    radius = (taps - 1) // 2
    peers = lax.axis_size("tensor")
    me = lax.axis_index("tensor")
    local = glu_input.shape[0] * frames
    everyone = local * lax.axis_size("dp") * peers
    flat_grad = out_grad.reshape(-1, width)
    group_grad = lax.all_gather(flat_grad, "tensor", axis=0, tiled=True)
    own_columns = jnp.einsum("fd,cd->fc", group_grad, proj_weight, preferred_element_type=jnp.float32)
    grad_act = lax.all_to_all(own_columns, "tensor", split_axis=0, concat_axis=1, tiled=True)
    grad_act = grad_act.reshape(out_grad.shape)
    values = glu_input[..., :width].astype(jnp.float32)
    gates = jax.nn.sigmoid(glu_input[..., width:].astype(jnp.float32))
    gated = (values * gates).astype(jnp.bfloat16)
    padded = extended(gated, (("tensor", 1),), radius)
    conv_out = jnp.zeros(gated.shape, jnp.float32)
    for offset in range(taps):
        conv_out = conv_out + depth_kernel[offset] * padded[:, offset : offset + frames, :]
    mean_local = jnp.sum(conv_out, axis=(0, 1)) / local
    dev_local = conv_out - mean_local
    spread_local = jnp.sum(dev_local * dev_local, axis=(0, 1))
    if all(is_power_of_two(lax.axis_size(a)) for a in ("dp", "tensor")):
        average, spread = all_moments(mean_local, spread_local, float(local), ("dp", "tensor"))
        variance = spread / everyone
    else:
        average = lax.psum(jnp.sum(conv_out, axis=(0, 1)), ("dp", "tensor")) / everyone
        centred0 = conv_out - average
        variance = lax.psum(jnp.sum(centred0 * centred0, axis=(0, 1)), ("dp", "tensor")) / everyone
    centred = conv_out - average
    inverse = lax.rsqrt(variance + epsilon)
    normed = centred * inverse
    affine = norm_scale * normed + norm_shift
    sig_affine = jax.nn.sigmoid(affine)
    activated = (affine * sig_affine).astype(jnp.bfloat16)
    flat_act = activated.reshape(-1, width)
    group_act = lax.all_to_all(flat_act, "tensor", split_axis=1, concat_axis=0, tiled=True)
    local_grad = jnp.einsum("fc,fd->cd", group_act, group_grad, preferred_element_type=jnp.float32)
    grad_affine = grad_act * (sig_affine + affine * sig_affine * (1.0 - sig_affine))
    sums = jnp.stack([jnp.sum(grad_affine, axis=(0, 1)), jnp.sum(grad_affine * normed, axis=(0, 1))])
    sums = all_sum(sums, ("dp", "tensor"))
    shift_grad, scale_grad = sums[0], sums[1]
    grad_conv = (
        norm_scale
        * inverse
        * (grad_affine - shift_grad / everyone - normed * scale_grad / everyone)
    ).astype(jnp.bfloat16)
    grad_pad = extended(grad_conv, (("tensor", 1),), radius)
    grad_gated = jnp.zeros(gated.shape, jnp.float32)
    for offset in range(taps):
        begin = 2 * radius - offset
        grad_gated = grad_gated + depth_kernel[offset] * grad_pad[:, begin : begin + frames, :]
    grad_wide = grad_conv.astype(jnp.float32)
    kernel_terms = jnp.stack(
        [
            jnp.sum(
                padded[:, offset : offset + frames, :].astype(jnp.float32) * grad_wide, axis=(0, 1)
            )
            for offset in range(taps)
        ]
    )
    local_grad, kernel_terms = lax.optimization_barrier((local_grad, kernel_terms))
    weight_grad = rows_sum(local_grad, "dp")
    kernel_grad = all_sum(kernel_terms, ("dp", "tensor"))
    input_grad = jnp.concatenate(
        [grad_gated * gates, grad_gated * values * gates * (1.0 - gates)], axis=-1
    ).astype(jnp.bfloat16)
    full_weight = gather_weight(proj_weight)
    conv_output = jnp.einsum(
        "btc,cd->btd", activated, full_weight, preferred_element_type=jnp.float32
    ).astype(jnp.bfloat16)
    return (conv_output, input_grad, weight_grad, kernel_grad, scale_grad, shift_grad)


def solution(mesh):
    in_specs = (P("dp", "tensor", None), P(), P(), P(), P("tensor", None), P("dp", "tensor", None))
    out_specs = (P("dp", "tensor", None), P("dp", "tensor", None), P("tensor", None), P(), P(), P())
    return jax.shard_map(
        on_device, mesh=mesh, in_specs=in_specs, out_specs=out_specs, check_vma=False
    )
```

```python
import jax
import jax.numpy as jnp
from jax import lax
from jax.sharding import PartitionSpec as P

epsilon = 1e-05


def extended(array, sides, width):
    for axis, dim in sides:
        peers, length = (lax.axis_size(axis), array.shape[dim])
        up = [(i, (i + 1) % peers) for i in range(peers - 1)]
        down = [(j, i) for i, j in up]
        last = lax.slice_in_dim(array, length - width, length, axis=dim)
        leading = lax.slice_in_dim(array, 0, width, axis=dim)
        before = lax.ppermute(last, axis, up)
        after = lax.ppermute(leading, axis, down)
        array = jnp.concatenate([before, array, after], axis=dim)
    return array


def is_power_of_two(n):
    return n > 0 and (n & (n - 1)) == 0


def all_sum(x, axes):
    for axis in axes:
        peers = lax.axis_size(axis)
        if not is_power_of_two(peers):
            x = lax.psum(x, axis)
            continue
        step = 1
        while step < peers:
            x = x + lax.ppermute(x, axis, [(i, i ^ step) for i in range(peers)])
            step *= 2
    return x


def all_moments(mean, spread, count, axes):
    for axis in axes:
        peers = lax.axis_size(axis)
        step = 1
        while step < peers:
            other = lax.ppermute(jnp.stack([mean, spread]), axis, [(i, i ^ step) for i in range(peers)])
            delta = other[0] - mean
            mean = (mean + other[0]) * 0.5
            spread = (spread + other[1]) + delta * delta * (count * 0.5)
            count = count * 2
            step *= 2
    return mean, spread


def rows_sum(x, axis):
    peers = lax.axis_size(axis)
    if not is_power_of_two(peers) or x.shape[0] % peers:
        return lax.psum(x, axis)
    me = lax.axis_index(axis)
    bits = []
    step = 1
    while step < peers:
        bit = lax.rem(me // step, 2)
        half = x.shape[0] // 2
        keep = lax.dynamic_slice_in_dim(x, bit * half, half, axis=0)
        give = lax.dynamic_slice_in_dim(x, (1 - bit) * half, half, axis=0)
        x = keep + lax.ppermute(give, axis, [(i, i ^ step) for i in range(peers)])
        bits.append((step, bit))
        step *= 2
    for step, bit in reversed(bits):
        other = lax.ppermute(x, axis, [(i, i ^ step) for i in range(peers)])
        x = jnp.where(bit == 0, jnp.concatenate([x, other]), jnp.concatenate([other, x]))
    return x


def gather_weight(block):
    if lax.axis_size("dp") % 2:
        return lax.all_gather(block, "tensor", axis=0, tiled=True)
    peers = lax.axis_size("tensor")
    half = block.shape[0] // 2
    core = lax.rem(lax.axis_index("dp"), 2)
    mine = lax.dynamic_slice_in_dim(block, core * half, half, axis=0)
    held = lax.all_gather(mine, "tensor", axis=0, tiled=False)
    other = lax.ppermute(held, "dp", [(i, i ^ 1) for i in range(lax.axis_size("dp"))])
    first = jnp.where(core == 0, held, other)
    second = jnp.where(core == 0, other, held)
    return jnp.concatenate([first, second], axis=1).reshape(peers * block.shape[0], block.shape[1])


def on_device(glu_input, depth_kernel, norm_scale, norm_shift, proj_weight, out_grad):
    width = proj_weight.shape[1]
    rows = proj_weight.shape[0]
    frames = glu_input.shape[1]
    taps = depth_kernel.shape[0]
    radius = (taps - 1) // 2
    peers = lax.axis_size("tensor")
    me = lax.axis_index("tensor")
    local = glu_input.shape[0] * frames
    everyone = local * lax.axis_size("dp") * peers
    flat_grad = out_grad.reshape(-1, width)
    group_grad = lax.all_gather(flat_grad, "tensor", axis=0, tiled=True)
    own_columns = jnp.einsum("fd,cd->fc", group_grad, proj_weight, preferred_element_type=jnp.float32)
    grad_act = lax.all_to_all(own_columns, "tensor", split_axis=0, concat_axis=1, tiled=True)
    grad_act = grad_act.reshape(out_grad.shape)
    values = glu_input[..., :width].astype(jnp.float32)
    gates = jax.nn.sigmoid(glu_input[..., width:].astype(jnp.float32))
    gated = (values * gates).astype(jnp.bfloat16)
    padded = extended(gated, (("tensor", 1),), radius)
    conv_out = jnp.zeros(gated.shape, jnp.float32)
    for offset in range(taps):
        conv_out = conv_out + depth_kernel[offset] * padded[:, offset : offset + frames, :]
    mean_local = jnp.sum(conv_out, axis=(0, 1)) / local
    dev_local = conv_out - mean_local
    spread_local = jnp.sum(dev_local * dev_local, axis=(0, 1))
    if all(is_power_of_two(lax.axis_size(a)) for a in ("dp", "tensor")):
        average, spread = all_moments(mean_local, spread_local, float(local), ("dp", "tensor"))
        variance = spread / everyone
    else:
        average = lax.psum(jnp.sum(conv_out, axis=(0, 1)), ("dp", "tensor")) / everyone
        centred0 = conv_out - average
        variance = lax.psum(jnp.sum(centred0 * centred0, axis=(0, 1)), ("dp", "tensor")) / everyone
    centred = conv_out - average
    inverse = lax.rsqrt(variance + epsilon)
    normed = centred * inverse
    affine = norm_scale * normed + norm_shift
    sig_affine = jax.nn.sigmoid(affine)
    activated = (affine * sig_affine).astype(jnp.bfloat16)
    flat_act = activated.reshape(-1, width)
    group_act = lax.all_to_all(flat_act, "tensor", split_axis=1, concat_axis=0, tiled=True)
    local_grad = jnp.einsum("fc,fd->cd", group_act, group_grad, preferred_element_type=jnp.float32)
    grad_affine = grad_act * (sig_affine + affine * sig_affine * (1.0 - sig_affine))
    sums = jnp.stack([jnp.sum(grad_affine, axis=(0, 1)), jnp.sum(grad_affine * normed, axis=(0, 1))])
    sums = all_sum(sums, ("dp", "tensor"))
    shift_grad, scale_grad = sums[0], sums[1]
    grad_conv = (
        norm_scale
        * inverse
        * (grad_affine - shift_grad / everyone - normed * scale_grad / everyone)
    ).astype(jnp.bfloat16)
    grad_pad = extended(grad_conv, (("tensor", 1),), radius)
    grad_gated = jnp.zeros(gated.shape, jnp.float32)
    for offset in range(taps):
        begin = 2 * radius - offset
        grad_gated = grad_gated + depth_kernel[offset] * grad_pad[:, begin : begin + frames, :]
    grad_wide = grad_conv.astype(jnp.float32)
    kernel_terms = jnp.stack(
        [
            jnp.sum(
                padded[:, offset : offset + frames, :].astype(jnp.float32) * grad_wide, axis=(0, 1)
            )
            for offset in range(taps)
        ]
    )
    local_grad, kernel_terms = lax.optimization_barrier((local_grad, kernel_terms))
    weight_grad = rows_sum(local_grad, "dp")
    kernel_grad = all_sum(kernel_terms, ("dp", "tensor"))
    input_grad = jnp.concatenate(
        [grad_gated * gates, grad_gated * values * gates * (1.0 - gates)], axis=-1
    ).astype(jnp.bfloat16)
    full_weight = gather_weight(proj_weight)
    late_act, kernel_grad = lax.optimization_barrier((activated, kernel_grad))
    conv_output = jnp.einsum(
        "btc,cd->btd", late_act, full_weight, preferred_element_type=jnp.float32
    ).astype(jnp.bfloat16)
    return (conv_output, input_grad, weight_grad, kernel_grad, scale_grad, shift_grad)


def solution(mesh):
    in_specs = (P("dp", "tensor", None), P(), P(), P(), P("tensor", None), P("dp", "tensor", None))
    out_specs = (P("dp", "tensor", None), P("dp", "tensor", None), P("tensor", None), P(), P(), P())
    return jax.shard_map(
        on_device, mesh=mesh, in_specs=in_specs, out_specs=out_specs, check_vma=False
    )
```

```python
import jax
import jax.numpy as jnp
from jax import lax
from jax.sharding import PartitionSpec as P

epsilon = 1e-05


def extended(array, sides, width):
    for axis, dim in sides:
        peers, length = (lax.axis_size(axis), array.shape[dim])
        up = [(i, (i + 1) % peers) for i in range(peers - 1)]
        down = [(j, i) for i, j in up]
        last = lax.slice_in_dim(array, length - width, length, axis=dim)
        leading = lax.slice_in_dim(array, 0, width, axis=dim)
        before = lax.ppermute(last, axis, up)
        after = lax.ppermute(leading, axis, down)
        array = jnp.concatenate([before, array, after], axis=dim)
    return array


def is_power_of_two(n):
    return n > 0 and (n & (n - 1)) == 0


def all_sum(x, axes):
    for axis in axes:
        peers = lax.axis_size(axis)
        if not is_power_of_two(peers):
            x = lax.psum(x, axis)
            continue
        step = 1
        while step < peers:
            x = x + lax.ppermute(x, axis, [(i, i ^ step) for i in range(peers)])
            step *= 2
    return x


def all_moments(mean, spread, count, axes):
    for axis in axes:
        peers = lax.axis_size(axis)
        step = 1
        while step < peers:
            other = lax.ppermute(jnp.stack([mean, spread]), axis, [(i, i ^ step) for i in range(peers)])
            delta = other[0] - mean
            mean = (mean + other[0]) * 0.5
            spread = (spread + other[1]) + delta * delta * (count * 0.5)
            count = count * 2
            step *= 2
    return mean, spread


def rows_sum(x, axis):
    peers = lax.axis_size(axis)
    if not is_power_of_two(peers) or x.shape[0] % peers:
        return lax.psum(x, axis)
    me = lax.axis_index(axis)
    bits = []
    step = 1
    while step < peers:
        bit = lax.rem(me // step, 2)
        half = x.shape[0] // 2
        keep = lax.dynamic_slice_in_dim(x, bit * half, half, axis=0)
        give = lax.dynamic_slice_in_dim(x, (1 - bit) * half, half, axis=0)
        x = keep + lax.ppermute(give, axis, [(i, i ^ step) for i in range(peers)])
        bits.append((step, bit))
        step *= 2
    for step, bit in reversed(bits):
        other = lax.ppermute(x, axis, [(i, i ^ step) for i in range(peers)])
        x = jnp.where(bit == 0, jnp.concatenate([x, other]), jnp.concatenate([other, x]))
    return x


def gather_weight(block):
    if lax.axis_size("dp") % 2:
        return lax.all_gather(block, "tensor", axis=0, tiled=True)
    peers = lax.axis_size("tensor")
    half = block.shape[0] // 2
    core = lax.rem(lax.axis_index("dp"), 2)
    mine = lax.dynamic_slice_in_dim(block, core * half, half, axis=0)
    held = lax.all_gather(mine, "tensor", axis=0, tiled=False)
    other = lax.ppermute(held, "dp", [(i, i ^ 1) for i in range(lax.axis_size("dp"))])
    first = jnp.where(core == 0, held, other)
    second = jnp.where(core == 0, other, held)
    return jnp.concatenate([first, second], axis=1).reshape(peers * block.shape[0], block.shape[1])


def on_device(glu_input, depth_kernel, norm_scale, norm_shift, proj_weight, out_grad):
    width = proj_weight.shape[1]
    rows = proj_weight.shape[0]
    frames = glu_input.shape[1]
    taps = depth_kernel.shape[0]
    radius = (taps - 1) // 2
    peers = lax.axis_size("tensor")
    me = lax.axis_index("tensor")
    local = glu_input.shape[0] * frames
    everyone = local * lax.axis_size("dp") * peers
    flat_grad = out_grad.reshape(-1, width)
    group_grad = lax.all_gather(flat_grad, "tensor", axis=0, tiled=True)
    values = glu_input[..., :width].astype(jnp.float32)
    gates = jax.nn.sigmoid(glu_input[..., width:].astype(jnp.float32))
    gated = (values * gates).astype(jnp.bfloat16)
    padded = extended(gated, (("tensor", 1),), radius)
    conv_out = jnp.zeros(gated.shape, jnp.float32)
    for offset in range(taps):
        conv_out = conv_out + depth_kernel[offset] * padded[:, offset : offset + frames, :]
    mean_local = jnp.sum(conv_out, axis=(0, 1)) / local
    dev_local = conv_out - mean_local
    spread_local = jnp.sum(dev_local * dev_local, axis=(0, 1))
    if all(is_power_of_two(lax.axis_size(a)) for a in ("dp", "tensor")):
        average, spread = all_moments(mean_local, spread_local, float(local), ("dp", "tensor"))
        variance = spread / everyone
    else:
        average = lax.psum(jnp.sum(conv_out, axis=(0, 1)), ("dp", "tensor")) / everyone
        centred0 = conv_out - average
        variance = lax.psum(jnp.sum(centred0 * centred0, axis=(0, 1)), ("dp", "tensor")) / everyone
    group_grad, average = lax.optimization_barrier((group_grad, average))
    own_columns = jnp.einsum("fd,cd->fc", group_grad, proj_weight, preferred_element_type=jnp.float32)
    grad_act = lax.all_to_all(own_columns, "tensor", split_axis=0, concat_axis=1, tiled=True)
    grad_act = grad_act.reshape(out_grad.shape)
    centred = conv_out - average
    inverse = lax.rsqrt(variance + epsilon)
    normed = centred * inverse
    affine = norm_scale * normed + norm_shift
    sig_affine = jax.nn.sigmoid(affine)
    activated = (affine * sig_affine).astype(jnp.bfloat16)
    flat_act = activated.reshape(-1, width)
    group_act = lax.all_to_all(flat_act, "tensor", split_axis=1, concat_axis=0, tiled=True)
    local_grad = jnp.einsum("fc,fd->cd", group_act, group_grad, preferred_element_type=jnp.float32)
    grad_affine = grad_act * (sig_affine + affine * sig_affine * (1.0 - sig_affine))
    sums = jnp.stack([jnp.sum(grad_affine, axis=(0, 1)), jnp.sum(grad_affine * normed, axis=(0, 1))])
    sums = all_sum(sums, ("dp", "tensor"))
    shift_grad, scale_grad = sums[0], sums[1]
    grad_conv = (
        norm_scale
        * inverse
        * (grad_affine - shift_grad / everyone - normed * scale_grad / everyone)
    ).astype(jnp.bfloat16)
    grad_pad = extended(grad_conv, (("tensor", 1),), radius)
    grad_gated = jnp.zeros(gated.shape, jnp.float32)
    for offset in range(taps):
        begin = 2 * radius - offset
        grad_gated = grad_gated + depth_kernel[offset] * grad_pad[:, begin : begin + frames, :]
    grad_wide = grad_conv.astype(jnp.float32)
    kernel_terms = jnp.stack(
        [
            jnp.sum(
                padded[:, offset : offset + frames, :].astype(jnp.float32) * grad_wide, axis=(0, 1)
            )
            for offset in range(taps)
        ]
    )
    local_grad, kernel_terms = lax.optimization_barrier((local_grad, kernel_terms))
    weight_grad = rows_sum(local_grad, "dp")
    kernel_grad = all_sum(kernel_terms, ("dp", "tensor"))
    input_grad = jnp.concatenate(
        [grad_gated * gates, grad_gated * values * gates * (1.0 - gates)], axis=-1
    ).astype(jnp.bfloat16)
    full_weight = gather_weight(proj_weight)
    conv_output = jnp.einsum(
        "btc,cd->btd", activated, full_weight, preferred_element_type=jnp.float32
    ).astype(jnp.bfloat16)
    return (conv_output, input_grad, weight_grad, kernel_grad, scale_grad, shift_grad)


def solution(mesh):
    in_specs = (P("dp", "tensor", None), P(), P(), P(), P("tensor", None), P("dp", "tensor", None))
    out_specs = (P("dp", "tensor", None), P("dp", "tensor", None), P("tensor", None), P(), P(), P())
    return jax.shard_map(
        on_device, mesh=mesh, in_specs=in_specs, out_specs=out_specs, check_vma=False
    )
```

```python
import jax
import jax.numpy as jnp
from jax import lax
from jax.sharding import PartitionSpec as P

epsilon = 1e-05


def extended(array, sides, width):
    for axis, dim in sides:
        peers, length = (lax.axis_size(axis), array.shape[dim])
        up = [(i, (i + 1) % peers) for i in range(peers - 1)]
        down = [(j, i) for i, j in up]
        last = lax.slice_in_dim(array, length - width, length, axis=dim)
        leading = lax.slice_in_dim(array, 0, width, axis=dim)
        before = lax.ppermute(last, axis, up)
        after = lax.ppermute(leading, axis, down)
        array = jnp.concatenate([before, array, after], axis=dim)
    return array


def is_power_of_two(n):
    return n > 0 and (n & (n - 1)) == 0


def all_sum(x, axes):
    for axis in axes:
        peers = lax.axis_size(axis)
        if not is_power_of_two(peers):
            x = lax.psum(x, axis)
            continue
        step = 1
        while step < peers:
            x = x + lax.ppermute(x, axis, [(i, i ^ step) for i in range(peers)])
            step *= 2
    return x


def all_moments(mean, spread, count, axes):
    for axis in axes:
        peers = lax.axis_size(axis)
        step = 1
        while step < peers:
            other = lax.ppermute(jnp.stack([mean, spread]), axis, [(i, i ^ step) for i in range(peers)])
            delta = other[0] - mean
            mean = (mean + other[0]) * 0.5
            spread = (spread + other[1]) + delta * delta * (count * 0.5)
            count = count * 2
            step *= 2
    return mean, spread


def rows_sum(x, axis):
    peers = lax.axis_size(axis)
    if not is_power_of_two(peers) or x.shape[0] % peers:
        return lax.psum(x, axis)
    me = lax.axis_index(axis)
    bits = []
    step = 1
    while step < peers:
        bit = lax.rem(me // step, 2)
        half = x.shape[0] // 2
        keep = lax.dynamic_slice_in_dim(x, bit * half, half, axis=0)
        give = lax.dynamic_slice_in_dim(x, (1 - bit) * half, half, axis=0)
        x = keep + lax.ppermute(give, axis, [(i, i ^ step) for i in range(peers)])
        bits.append((step, bit))
        step *= 2
    for step, bit in reversed(bits):
        other = lax.ppermute(x, axis, [(i, i ^ step) for i in range(peers)])
        x = jnp.where(bit == 0, jnp.concatenate([x, other]), jnp.concatenate([other, x]))
    return x


def gather_weight(block, anchor):
    if lax.axis_size("dp") % 2:
        return lax.all_gather(block, "tensor", axis=0, tiled=True), anchor
    peers = lax.axis_size("tensor")
    half = block.shape[0] // 2
    core = lax.rem(lax.axis_index("dp"), 2)
    mine = lax.dynamic_slice_in_dim(block, core * half, half, axis=0)
    held = lax.all_gather(mine, "tensor", axis=0, tiled=False)
    held, anchor = lax.optimization_barrier((held, anchor))
    other = lax.ppermute(held, "dp", [(i, i ^ 1) for i in range(lax.axis_size("dp"))])
    first = jnp.where(core == 0, held, other)
    second = jnp.where(core == 0, other, held)
    return jnp.concatenate([first, second], axis=1).reshape(peers * block.shape[0], block.shape[1]), anchor


def on_device(glu_input, depth_kernel, norm_scale, norm_shift, proj_weight, out_grad):
    width = proj_weight.shape[1]
    rows = proj_weight.shape[0]
    frames = glu_input.shape[1]
    taps = depth_kernel.shape[0]
    radius = (taps - 1) // 2
    peers = lax.axis_size("tensor")
    me = lax.axis_index("tensor")
    local = glu_input.shape[0] * frames
    everyone = local * lax.axis_size("dp") * peers
    flat_grad = out_grad.reshape(-1, width)
    group_grad = lax.all_gather(flat_grad, "tensor", axis=0, tiled=True)
    values = glu_input[..., :width].astype(jnp.float32)
    gates = jax.nn.sigmoid(glu_input[..., width:].astype(jnp.float32))
    gated = (values * gates).astype(jnp.bfloat16)
    padded = extended(gated, (("tensor", 1),), radius)
    conv_out = jnp.zeros(gated.shape, jnp.float32)
    for offset in range(taps):
        conv_out = conv_out + depth_kernel[offset] * padded[:, offset : offset + frames, :]
    mean_local = jnp.sum(conv_out, axis=(0, 1)) / local
    dev_local = conv_out - mean_local
    spread_local = jnp.sum(dev_local * dev_local, axis=(0, 1))
    if all(is_power_of_two(lax.axis_size(a)) for a in ("dp", "tensor")):
        average, spread = all_moments(mean_local, spread_local, float(local), ("dp", "tensor"))
        variance = spread / everyone
    else:
        average = lax.psum(jnp.sum(conv_out, axis=(0, 1)), ("dp", "tensor")) / everyone
        centred0 = conv_out - average
        variance = lax.psum(jnp.sum(centred0 * centred0, axis=(0, 1)), ("dp", "tensor")) / everyone
    group_grad, average = lax.optimization_barrier((group_grad, average))
    own_columns = jnp.einsum("fd,cd->fc", group_grad, proj_weight, preferred_element_type=jnp.float32)
    grad_act = lax.all_to_all(own_columns, "tensor", split_axis=0, concat_axis=1, tiled=True)
    grad_act = grad_act.reshape(out_grad.shape)
    centred = conv_out - average
    inverse = lax.rsqrt(variance + epsilon)
    normed = centred * inverse
    affine = norm_scale * normed + norm_shift
    sig_affine = jax.nn.sigmoid(affine)
    activated = (affine * sig_affine).astype(jnp.bfloat16)
    flat_act = activated.reshape(-1, width)
    group_act = lax.all_to_all(flat_act, "tensor", split_axis=1, concat_axis=0, tiled=True)
    local_grad = jnp.einsum("fc,fd->cd", group_act, group_grad, preferred_element_type=jnp.float32)
    grad_affine = grad_act * (sig_affine + affine * sig_affine * (1.0 - sig_affine))
    sums = jnp.stack([jnp.sum(grad_affine, axis=(0, 1)), jnp.sum(grad_affine * normed, axis=(0, 1))])
    sums = all_sum(sums, ("dp", "tensor"))
    shift_grad, scale_grad = sums[0], sums[1]
    grad_conv = (
        norm_scale
        * inverse
        * (grad_affine - shift_grad / everyone - normed * scale_grad / everyone)
    ).astype(jnp.bfloat16)
    grad_pad = extended(grad_conv, (("tensor", 1),), radius)
    grad_gated = jnp.zeros(gated.shape, jnp.float32)
    for offset in range(taps):
        begin = 2 * radius - offset
        grad_gated = grad_gated + depth_kernel[offset] * grad_pad[:, begin : begin + frames, :]
    grad_wide = grad_conv.astype(jnp.float32)
    kernel_terms = jnp.stack(
        [
            jnp.sum(
                padded[:, offset : offset + frames, :].astype(jnp.float32) * grad_wide, axis=(0, 1)
            )
            for offset in range(taps)
        ]
    )
    local_grad, kernel_terms = lax.optimization_barrier((local_grad, kernel_terms))
    weight_grad = rows_sum(local_grad, "dp")
    kernel_grad = all_sum(kernel_terms, ("dp", "tensor"))
    full_weight, kernel_grad = gather_weight(proj_weight, kernel_grad)
    input_grad = jnp.concatenate(
        [grad_gated * gates, grad_gated * values * gates * (1.0 - gates)], axis=-1
    ).astype(jnp.bfloat16)
    conv_output = jnp.einsum(
        "btc,cd->btd", activated, full_weight, preferred_element_type=jnp.float32
    ).astype(jnp.bfloat16)
    return (conv_output, input_grad, weight_grad, kernel_grad, scale_grad, shift_grad)


def solution(mesh):
    in_specs = (P("dp", "tensor", None), P(), P(), P(), P("tensor", None), P("dp", "tensor", None))
    out_specs = (P("dp", "tensor", None), P("dp", "tensor", None), P("tensor", None), P(), P(), P())
    return jax.shard_map(
        on_device, mesh=mesh, in_specs=in_specs, out_specs=out_specs, check_vma=False
    )
```

```python
import jax
import jax.numpy as jnp
from jax import lax
from jax.sharding import PartitionSpec as P

epsilon = 1e-05


def extended(array, sides, width):
    for axis, dim in sides:
        peers, length = (lax.axis_size(axis), array.shape[dim])
        up = [(i, (i + 1) % peers) for i in range(peers - 1)]
        down = [(j, i) for i, j in up]
        last = lax.slice_in_dim(array, length - width, length, axis=dim)
        leading = lax.slice_in_dim(array, 0, width, axis=dim)
        before = lax.ppermute(last, axis, up)
        after = lax.ppermute(leading, axis, down)
        array = jnp.concatenate([before, array, after], axis=dim)
    return array


def is_power_of_two(n):
    return n > 0 and (n & (n - 1)) == 0


def all_sum(x, axes):
    for axis in axes:
        peers = lax.axis_size(axis)
        if not is_power_of_two(peers):
            x = lax.psum(x, axis)
            continue
        step = 1
        while step < peers:
            x = x + lax.ppermute(x, axis, [(i, i ^ step) for i in range(peers)])
            step *= 2
    return x


def all_moments(mean, spread, count, axes):
    for axis in axes:
        peers = lax.axis_size(axis)
        step = 1
        while step < peers:
            other = lax.ppermute(jnp.stack([mean, spread]), axis, [(i, i ^ step) for i in range(peers)])
            delta = other[0] - mean
            mean = (mean + other[0]) * 0.5
            spread = (spread + other[1]) + delta * delta * (count * 0.5)
            count = count * 2
            step *= 2
    return mean, spread


def rows_sum(x, axis):
    peers = lax.axis_size(axis)
    if not is_power_of_two(peers) or x.shape[0] % peers:
        return lax.psum(x, axis)
    me = lax.axis_index(axis)
    bits = []
    step = 1
    while step < peers:
        bit = lax.rem(me // step, 2)
        half = x.shape[0] // 2
        keep = lax.dynamic_slice_in_dim(x, bit * half, half, axis=0)
        give = lax.dynamic_slice_in_dim(x, (1 - bit) * half, half, axis=0)
        x = keep + lax.ppermute(give, axis, [(i, i ^ step) for i in range(peers)])
        bits.append((step, bit))
        step *= 2
    for step, bit in reversed(bits):
        other = lax.ppermute(x, axis, [(i, i ^ step) for i in range(peers)])
        x = jnp.where(bit == 0, jnp.concatenate([x, other]), jnp.concatenate([other, x]))
    return x


def gather_weight(block):
    group = lax.axis_size("dp")
    if group % 4 or block.shape[0] % 4:
        return lax.all_gather(block, "tensor", axis=0, tiled=True)
    peers = lax.axis_size("tensor")
    piece = block.shape[0] // 4
    where = lax.axis_index("dp")
    low, high = lax.rem(where, 2), lax.rem(where // 2, 2)
    mine = lax.dynamic_slice_in_dim(block, (high * 2 + low) * piece, piece, axis=0)
    held = lax.all_gather(mine, "tensor", axis=0, tiled=False)
    other = lax.ppermute(held, "dp", [(i, i ^ 2) for i in range(group)])
    pair = jnp.stack([jnp.where(high == 0, held, other), jnp.where(high == 0, other, held)], axis=1)
    other = lax.ppermute(pair, "dp", [(i, i ^ 1) for i in range(group)])
    whole = jnp.stack([jnp.where(low == 0, pair, other), jnp.where(low == 0, other, pair)], axis=2)
    return whole.reshape(peers * block.shape[0], block.shape[1])


def on_device(glu_input, depth_kernel, norm_scale, norm_shift, proj_weight, out_grad):
    width = proj_weight.shape[1]
    rows = proj_weight.shape[0]
    frames = glu_input.shape[1]
    taps = depth_kernel.shape[0]
    radius = (taps - 1) // 2
    peers = lax.axis_size("tensor")
    me = lax.axis_index("tensor")
    local = glu_input.shape[0] * frames
    everyone = local * lax.axis_size("dp") * peers
    flat_grad = out_grad.reshape(-1, width)
    group_grad = lax.all_gather(flat_grad, "tensor", axis=0, tiled=True)
    values = glu_input[..., :width].astype(jnp.float32)
    gates = jax.nn.sigmoid(glu_input[..., width:].astype(jnp.float32))
    gated = (values * gates).astype(jnp.bfloat16)
    padded = extended(gated, (("tensor", 1),), radius)
    conv_out = jnp.zeros(gated.shape, jnp.float32)
    for offset in range(taps):
        conv_out = conv_out + depth_kernel[offset] * padded[:, offset : offset + frames, :]
    mean_local = jnp.sum(conv_out, axis=(0, 1)) / local
    dev_local = conv_out - mean_local
    spread_local = jnp.sum(dev_local * dev_local, axis=(0, 1))
    if all(is_power_of_two(lax.axis_size(a)) for a in ("dp", "tensor")):
        average, spread = all_moments(mean_local, spread_local, float(local), ("dp", "tensor"))
        variance = spread / everyone
    else:
        average = lax.psum(jnp.sum(conv_out, axis=(0, 1)), ("dp", "tensor")) / everyone
        centred0 = conv_out - average
        variance = lax.psum(jnp.sum(centred0 * centred0, axis=(0, 1)), ("dp", "tensor")) / everyone
    group_grad, average = lax.optimization_barrier((group_grad, average))
    own_columns = jnp.einsum("fd,cd->fc", group_grad, proj_weight, preferred_element_type=jnp.float32)
    grad_act = lax.all_to_all(own_columns, "tensor", split_axis=0, concat_axis=1, tiled=True)
    grad_act = grad_act.reshape(out_grad.shape)
    centred = conv_out - average
    inverse = lax.rsqrt(variance + epsilon)
    normed = centred * inverse
    affine = norm_scale * normed + norm_shift
    sig_affine = jax.nn.sigmoid(affine)
    activated = (affine * sig_affine).astype(jnp.bfloat16)
    flat_act = activated.reshape(-1, width)
    group_act = lax.all_to_all(flat_act, "tensor", split_axis=1, concat_axis=0, tiled=True)
    local_grad = jnp.einsum("fc,fd->cd", group_act, group_grad, preferred_element_type=jnp.float32)
    grad_affine = grad_act * (sig_affine + affine * sig_affine * (1.0 - sig_affine))
    sums = jnp.stack([jnp.sum(grad_affine, axis=(0, 1)), jnp.sum(grad_affine * normed, axis=(0, 1))])
    sums = all_sum(sums, ("dp", "tensor"))
    shift_grad, scale_grad = sums[0], sums[1]
    grad_conv = (
        norm_scale
        * inverse
        * (grad_affine - shift_grad / everyone - normed * scale_grad / everyone)
    ).astype(jnp.bfloat16)
    grad_pad = extended(grad_conv, (("tensor", 1),), radius)
    grad_gated = jnp.zeros(gated.shape, jnp.float32)
    for offset in range(taps):
        begin = 2 * radius - offset
        grad_gated = grad_gated + depth_kernel[offset] * grad_pad[:, begin : begin + frames, :]
    grad_wide = grad_conv.astype(jnp.float32)
    kernel_terms = jnp.stack(
        [
            jnp.sum(
                padded[:, offset : offset + frames, :].astype(jnp.float32) * grad_wide, axis=(0, 1)
            )
            for offset in range(taps)
        ]
    )
    local_grad, kernel_terms = lax.optimization_barrier((local_grad, kernel_terms))
    weight_grad = rows_sum(local_grad, "dp")
    kernel_grad = all_sum(kernel_terms, ("dp", "tensor"))
    input_grad = jnp.concatenate(
        [grad_gated * gates, grad_gated * values * gates * (1.0 - gates)], axis=-1
    ).astype(jnp.bfloat16)
    full_weight = gather_weight(proj_weight)
    conv_output = jnp.einsum(
        "btc,cd->btd", activated, full_weight, preferred_element_type=jnp.float32
    ).astype(jnp.bfloat16)
    return (conv_output, input_grad, weight_grad, kernel_grad, scale_grad, shift_grad)


def solution(mesh):
    in_specs = (P("dp", "tensor", None), P(), P(), P(), P("tensor", None), P("dp", "tensor", None))
    out_specs = (P("dp", "tensor", None), P("dp", "tensor", None), P("tensor", None), P(), P(), P())
    return jax.shard_map(
        on_device, mesh=mesh, in_specs=in_specs, out_specs=out_specs, check_vma=False
    )
```

```python
import jax
import jax.numpy as jnp
from jax import lax
from jax.sharding import PartitionSpec as P

epsilon = 1e-05


def extended(array, sides, width):
    for axis, dim in sides:
        peers, length = (lax.axis_size(axis), array.shape[dim])
        up = [(i, (i + 1) % peers) for i in range(peers - 1)]
        down = [(j, i) for i, j in up]
        last = lax.slice_in_dim(array, length - width, length, axis=dim)
        leading = lax.slice_in_dim(array, 0, width, axis=dim)
        before = lax.ppermute(last, axis, up)
        after = lax.ppermute(leading, axis, down)
        array = jnp.concatenate([before, array, after], axis=dim)
    return array


def is_power_of_two(n):
    return n > 0 and (n & (n - 1)) == 0


def all_sum(x, axes):
    for axis in axes:
        peers = lax.axis_size(axis)
        if not is_power_of_two(peers):
            x = lax.psum(x, axis)
            continue
        step = 1
        while step < peers:
            x = x + lax.ppermute(x, axis, [(i, i ^ step) for i in range(peers)])
            step *= 2
    return x


def all_moments(mean, spread, count, axes):
    for axis in axes:
        peers = lax.axis_size(axis)
        step = 1
        while step < peers:
            other = lax.ppermute(jnp.stack([mean, spread]), axis, [(i, i ^ step) for i in range(peers)])
            delta = other[0] - mean
            mean = (mean + other[0]) * 0.5
            spread = (spread + other[1]) + delta * delta * (count * 0.5)
            count = count * 2
            step *= 2
    return mean, spread


def rows_sum(x, axis):
    peers = lax.axis_size(axis)
    if not is_power_of_two(peers) or x.shape[0] % peers:
        return lax.psum(x, axis)
    me = lax.axis_index(axis)
    bits = []
    step = 1
    while step < peers:
        bit = lax.rem(me // step, 2)
        half = x.shape[0] // 2
        keep = lax.dynamic_slice_in_dim(x, bit * half, half, axis=0)
        give = lax.dynamic_slice_in_dim(x, (1 - bit) * half, half, axis=0)
        x = keep + lax.ppermute(give, axis, [(i, i ^ step) for i in range(peers)])
        bits.append((step, bit))
        step *= 2
    for step, bit in reversed(bits):
        other = lax.ppermute(x, axis, [(i, i ^ step) for i in range(peers)])
        x = jnp.where(bit == 0, jnp.concatenate([x, other]), jnp.concatenate([other, x]))
    return x


def gather_weight(block, anchor):
    if lax.axis_size("dp") % 2:
        return lax.all_gather(block, "tensor", axis=0, tiled=True), anchor
    peers = lax.axis_size("tensor")
    half = block.shape[0] // 2
    core = lax.rem(lax.axis_index("dp"), 2)
    mine = lax.dynamic_slice_in_dim(block, core * half, half, axis=0)
    held = lax.all_gather(mine, "tensor", axis=0, tiled=False)
    held, anchor = lax.optimization_barrier((held, anchor))
    other = lax.ppermute(held, "dp", [(i, i ^ 1) for i in range(lax.axis_size("dp"))])
    first = jnp.where(core == 0, held, other)
    second = jnp.where(core == 0, other, held)
    return jnp.concatenate([first, second], axis=1).reshape(peers * block.shape[0], block.shape[1]), anchor


def on_device(glu_input, depth_kernel, norm_scale, norm_shift, proj_weight, out_grad):
    width = proj_weight.shape[1]
    rows = proj_weight.shape[0]
    frames = glu_input.shape[1]
    taps = depth_kernel.shape[0]
    radius = (taps - 1) // 2
    peers = lax.axis_size("tensor")
    me = lax.axis_index("tensor")
    local = glu_input.shape[0] * frames
    everyone = local * lax.axis_size("dp") * peers
    flat_grad = out_grad.reshape(-1, width)
    group_grad = lax.all_gather(flat_grad, "tensor", axis=0, tiled=True)
    values = glu_input[..., :width].astype(jnp.float32)
    gates = jax.nn.sigmoid(glu_input[..., width:].astype(jnp.float32))
    gated = (values * gates).astype(jnp.bfloat16)
    padded = extended(gated, (("tensor", 1),), radius)
    conv_out = jnp.zeros(gated.shape, jnp.float32)
    for offset in range(taps):
        conv_out = conv_out + depth_kernel[offset] * padded[:, offset : offset + frames, :]
    mean_local = jnp.sum(conv_out, axis=(0, 1)) / local
    dev_local = conv_out - mean_local
    spread_local = jnp.sum(dev_local * dev_local, axis=(0, 1))
    if all(is_power_of_two(lax.axis_size(a)) for a in ("dp", "tensor")):
        average, spread = all_moments(mean_local, spread_local, float(local), ("dp", "tensor"))
        variance = spread / everyone
    else:
        average = lax.psum(jnp.sum(conv_out, axis=(0, 1)), ("dp", "tensor")) / everyone
        centred0 = conv_out - average
        variance = lax.psum(jnp.sum(centred0 * centred0, axis=(0, 1)), ("dp", "tensor")) / everyone
    full_weight, average = gather_weight(proj_weight, average)
    centred = conv_out - average
    inverse = lax.rsqrt(variance + epsilon)
    normed = centred * inverse
    affine = norm_scale * normed + norm_shift
    sig_affine = jax.nn.sigmoid(affine)
    activated = (affine * sig_affine).astype(jnp.bfloat16)
    flat_act = activated.reshape(-1, width)
    group_act = lax.all_to_all(flat_act, "tensor", split_axis=1, concat_axis=0, tiled=True)
    local_grad = jnp.einsum("fc,fd->cd", group_act, group_grad, preferred_element_type=jnp.float32)
    conv_output = jnp.einsum(
        "btc,cd->btd", activated, full_weight, preferred_element_type=jnp.float32
    ).astype(jnp.bfloat16)
    grad_act = jnp.einsum("btd,cd->btc", out_grad, full_weight, preferred_element_type=jnp.float32)
    grad_affine = grad_act * (sig_affine + affine * sig_affine * (1.0 - sig_affine))
    sums = jnp.stack([jnp.sum(grad_affine, axis=(0, 1)), jnp.sum(grad_affine * normed, axis=(0, 1))])
    sums = all_sum(sums, ("dp", "tensor"))
    shift_grad, scale_grad = sums[0], sums[1]
    grad_conv = (
        norm_scale
        * inverse
        * (grad_affine - shift_grad / everyone - normed * scale_grad / everyone)
    ).astype(jnp.bfloat16)
    grad_pad = extended(grad_conv, (("tensor", 1),), radius)
    grad_gated = jnp.zeros(gated.shape, jnp.float32)
    for offset in range(taps):
        begin = 2 * radius - offset
        grad_gated = grad_gated + depth_kernel[offset] * grad_pad[:, begin : begin + frames, :]
    grad_wide = grad_conv.astype(jnp.float32)
    kernel_terms = jnp.stack(
        [
            jnp.sum(
                padded[:, offset : offset + frames, :].astype(jnp.float32) * grad_wide, axis=(0, 1)
            )
            for offset in range(taps)
        ]
    )
    local_grad, kernel_terms = lax.optimization_barrier((local_grad, kernel_terms))
    weight_grad = rows_sum(local_grad, "dp")
    kernel_grad = all_sum(kernel_terms, ("dp", "tensor"))
    input_grad = jnp.concatenate(
        [grad_gated * gates, grad_gated * values * gates * (1.0 - gates)], axis=-1
    ).astype(jnp.bfloat16)
    return (conv_output, input_grad, weight_grad, kernel_grad, scale_grad, shift_grad)


def solution(mesh):
    in_specs = (P("dp", "tensor", None), P(), P(), P(), P("tensor", None), P("dp", "tensor", None))
    out_specs = (P("dp", "tensor", None), P("dp", "tensor", None), P("tensor", None), P(), P(), P())
    return jax.shard_map(
        on_device, mesh=mesh, in_specs=in_specs, out_specs=out_specs, check_vma=False
    )
```

```python
import jax
import jax.numpy as jnp
from jax import lax
from jax.sharding import PartitionSpec as P

epsilon = 1e-05


def extended(array, sides, width):
    for axis, dim in sides:
        peers, length = (lax.axis_size(axis), array.shape[dim])
        up = [(i, (i + 1) % peers) for i in range(peers - 1)]
        down = [(j, i) for i, j in up]
        last = lax.slice_in_dim(array, length - width, length, axis=dim)
        leading = lax.slice_in_dim(array, 0, width, axis=dim)
        before = lax.ppermute(last, axis, up)
        after = lax.ppermute(leading, axis, down)
        array = jnp.concatenate([before, array, after], axis=dim)
    return array


def is_power_of_two(n):
    return n > 0 and (n & (n - 1)) == 0


def all_sum(x, axes):
    for axis in axes:
        peers = lax.axis_size(axis)
        if not is_power_of_two(peers):
            x = lax.psum(x, axis)
            continue
        step = 1
        while step < peers:
            x = x + lax.ppermute(x, axis, [(i, i ^ step) for i in range(peers)])
            step *= 2
    return x


def all_moments(mean, spread, count, axes):
    for axis in axes:
        peers = lax.axis_size(axis)
        step = 1
        while step < peers:
            other = lax.ppermute(jnp.stack([mean, spread]), axis, [(i, i ^ step) for i in range(peers)])
            delta = other[0] - mean
            mean = (mean + other[0]) * 0.5
            spread = (spread + other[1]) + delta * delta * (count * 0.5)
            count = count * 2
            step *= 2
    return mean, spread


def rows_sum(x, axis):
    peers = lax.axis_size(axis)
    if not is_power_of_two(peers) or x.shape[0] % peers:
        return lax.psum(x, axis)
    me = lax.axis_index(axis)
    bits = []
    step = 1
    while step < peers:
        bit = lax.rem(me // step, 2)
        half = x.shape[0] // 2
        keep = lax.dynamic_slice_in_dim(x, bit * half, half, axis=0)
        give = lax.dynamic_slice_in_dim(x, (1 - bit) * half, half, axis=0)
        x = keep + lax.ppermute(give, axis, [(i, i ^ step) for i in range(peers)])
        bits.append((step, bit))
        step *= 2
    for step, bit in reversed(bits):
        other = lax.ppermute(x, axis, [(i, i ^ step) for i in range(peers)])
        x = jnp.where(bit == 0, jnp.concatenate([x, other]), jnp.concatenate([other, x]))
    return x


def gather_weight(block):
    if lax.axis_size("dp") % 2:
        return lax.all_gather(block, "tensor", axis=0, tiled=True)
    peers = lax.axis_size("tensor")
    half = block.shape[0] // 2
    core = lax.rem(lax.axis_index("dp"), 2)
    mine = lax.dynamic_slice_in_dim(block, core * half, half, axis=0)
    held = lax.all_gather(mine, "tensor", axis=0, tiled=False)
    other = lax.ppermute(held, "dp", [(i, i ^ 1) for i in range(lax.axis_size("dp"))])
    first = jnp.where(core == 0, held, other)
    second = jnp.where(core == 0, other, held)
    return jnp.concatenate([first, second], axis=1).reshape(peers * block.shape[0], block.shape[1])


def on_device(glu_input, depth_kernel, norm_scale, norm_shift, proj_weight, out_grad):
    width = proj_weight.shape[1]
    rows = proj_weight.shape[0]
    frames = glu_input.shape[1]
    taps = depth_kernel.shape[0]
    radius = (taps - 1) // 2
    peers = lax.axis_size("tensor")
    me = lax.axis_index("tensor")
    local = glu_input.shape[0] * frames
    everyone = local * lax.axis_size("dp") * peers
    flat_grad = out_grad.reshape(-1, width)
    group_grad = lax.all_gather(flat_grad, "tensor", axis=0, tiled=True)
    values = glu_input[..., :width].astype(jnp.float32)
    gates = jax.nn.sigmoid(glu_input[..., width:].astype(jnp.float32))
    gated = (values * gates).astype(jnp.bfloat16)
    padded = extended(gated, (("tensor", 1),), radius)
    conv_out = jnp.zeros(gated.shape, jnp.float32)
    for offset in range(taps):
        conv_out = conv_out + depth_kernel[offset] * padded[:, offset : offset + frames, :]
    mean_local = jnp.sum(conv_out, axis=(0, 1)) / local
    dev_local = conv_out - mean_local
    spread_local = jnp.sum(dev_local * dev_local, axis=(0, 1))
    if all(is_power_of_two(lax.axis_size(a)) for a in ("dp", "tensor")):
        average, spread = all_moments(mean_local, spread_local, float(local), ("dp", "tensor"))
        variance = spread / everyone
    else:
        average = lax.psum(jnp.sum(conv_out, axis=(0, 1)), ("dp", "tensor")) / everyone
        centred0 = conv_out - average
        variance = lax.psum(jnp.sum(centred0 * centred0, axis=(0, 1)), ("dp", "tensor")) / everyone
    group_grad, average = lax.optimization_barrier((group_grad, average))
    own_columns = jnp.einsum("fd,cd->fc", group_grad, proj_weight, preferred_element_type=jnp.float32)
    grad_act = lax.all_to_all(own_columns, "tensor", split_axis=0, concat_axis=1, tiled=True)
    grad_act = grad_act.reshape(out_grad.shape)
    centred = conv_out - average
    inverse = lax.rsqrt(variance + epsilon)
    normed = centred * inverse
    affine = norm_scale * normed + norm_shift
    sig_affine = jax.nn.sigmoid(affine)
    activated = (affine * sig_affine).astype(jnp.bfloat16)
    flat_act = activated.reshape(-1, width)
    group_act = lax.all_to_all(flat_act, "tensor", split_axis=1, concat_axis=0, tiled=True)
    local_grad = jnp.einsum("fc,fd->cd", group_act, group_grad, preferred_element_type=jnp.float32)
    grad_affine = grad_act * (sig_affine + affine * sig_affine * (1.0 - sig_affine))
    sums = jnp.stack([jnp.sum(grad_affine, axis=(0, 1)), jnp.sum(grad_affine * normed, axis=(0, 1))])
    sums = all_sum(sums, ("dp", "tensor"))
    shift_grad, scale_grad = sums[0], sums[1]
    grad_conv = (
        norm_scale
        * inverse
        * (grad_affine - shift_grad / everyone - normed * scale_grad / everyone)
    ).astype(jnp.bfloat16)
    grad_pad = extended(grad_conv, (("tensor", 1),), radius)
    grad_gated = jnp.zeros(gated.shape, jnp.float32)
    for offset in range(taps):
        begin = 2 * radius - offset
        grad_gated = grad_gated + depth_kernel[offset] * grad_pad[:, begin : begin + frames, :]
    grad_wide = grad_conv.astype(jnp.float32)
    kernel_terms = jnp.stack(
        [
            jnp.sum(
                padded[:, offset : offset + frames, :].astype(jnp.float32) * grad_wide, axis=(0, 1)
            )
            for offset in range(taps)
        ]
    )
    weight_grad = rows_sum(local_grad, "dp")
    kernel_grad = all_sum(kernel_terms, ("dp", "tensor"))
    input_grad = jnp.concatenate(
        [grad_gated * gates, grad_gated * values * gates * (1.0 - gates)], axis=-1
    ).astype(jnp.bfloat16)
    full_weight = gather_weight(proj_weight)
    conv_output = jnp.einsum(
        "btc,cd->btd", activated, full_weight, preferred_element_type=jnp.float32
    ).astype(jnp.bfloat16)
    return (conv_output, input_grad, weight_grad, kernel_grad, scale_grad, shift_grad)


def solution(mesh):
    in_specs = (P("dp", "tensor", None), P(), P(), P(), P("tensor", None), P("dp", "tensor", None))
    out_specs = (P("dp", "tensor", None), P("dp", "tensor", None), P("tensor", None), P(), P(), P())
    return jax.shard_map(
        on_device, mesh=mesh, in_specs=in_specs, out_specs=out_specs, check_vma=False
    )
```

```python
import jax
import jax.numpy as jnp
from jax import lax
from jax.sharding import PartitionSpec as P

epsilon = 1e-05


def extended(array, sides, width):
    for axis, dim in sides:
        peers, length = (lax.axis_size(axis), array.shape[dim])
        up = [(i, (i + 1) % peers) for i in range(peers - 1)]
        down = [(j, i) for i, j in up]
        last = lax.slice_in_dim(array, length - width, length, axis=dim)
        leading = lax.slice_in_dim(array, 0, width, axis=dim)
        before = lax.ppermute(last, axis, up)
        after = lax.ppermute(leading, axis, down)
        array = jnp.concatenate([before, array, after], axis=dim)
    return array


def is_power_of_two(n):
    return n > 0 and (n & (n - 1)) == 0


def all_sum(x, axes):
    for axis in axes:
        peers = lax.axis_size(axis)
        if not is_power_of_two(peers):
            x = lax.psum(x, axis)
            continue
        step = 1
        while step < peers:
            x = x + lax.ppermute(x, axis, [(i, i ^ step) for i in range(peers)])
            step *= 2
    return x


def all_moments(mean, spread, count, axes):
    for axis in axes:
        peers = lax.axis_size(axis)
        step = 1
        while step < peers:
            other = lax.ppermute(jnp.stack([mean, spread]), axis, [(i, i ^ step) for i in range(peers)])
            delta = other[0] - mean
            mean = (mean + other[0]) * 0.5
            spread = (spread + other[1]) + delta * delta * (count * 0.5)
            count = count * 2
            step *= 2
    return mean, spread


def rows_sum(x, axis):
    peers = lax.axis_size(axis)
    if not is_power_of_two(peers) or x.shape[0] % peers:
        return lax.psum(x, axis)
    me = lax.axis_index(axis)
    bits = []
    step = 1
    while step < peers:
        bit = lax.rem(me // step, 2)
        half = x.shape[0] // 2
        keep = lax.dynamic_slice_in_dim(x, bit * half, half, axis=0)
        give = lax.dynamic_slice_in_dim(x, (1 - bit) * half, half, axis=0)
        x = keep + lax.ppermute(give, axis, [(i, i ^ step) for i in range(peers)])
        bits.append((step, bit))
        step *= 2
    for step, bit in reversed(bits):
        other = lax.ppermute(x, axis, [(i, i ^ step) for i in range(peers)])
        x = jnp.where(bit == 0, jnp.concatenate([x, other]), jnp.concatenate([other, x]))
    return x


def gather_weight(block):
    if lax.axis_size("dp") % 2:
        return lax.all_gather(block, "tensor", axis=0, tiled=True)
    peers = lax.axis_size("tensor")
    half = block.shape[0] // 2
    core = lax.rem(lax.axis_index("dp"), 2)
    mine = lax.dynamic_slice_in_dim(block, core * half, half, axis=0)
    held = lax.all_gather(mine, "tensor", axis=0, tiled=False)
    other = lax.ppermute(held, "dp", [(i, i ^ 1) for i in range(lax.axis_size("dp"))])
    first = jnp.where(core == 0, held, other)
    second = jnp.where(core == 0, other, held)
    return jnp.concatenate([first, second], axis=1).reshape(peers * block.shape[0], block.shape[1])


def on_device(glu_input, depth_kernel, norm_scale, norm_shift, proj_weight, out_grad):
    width = proj_weight.shape[1]
    rows = proj_weight.shape[0]
    frames = glu_input.shape[1]
    taps = depth_kernel.shape[0]
    radius = (taps - 1) // 2
    peers = lax.axis_size("tensor")
    me = lax.axis_index("tensor")
    local = glu_input.shape[0] * frames
    everyone = local * lax.axis_size("dp") * peers
    flat_grad = out_grad.reshape(-1, width)
    group_grad = lax.all_gather(flat_grad, "tensor", axis=0, tiled=True)
    values = glu_input[..., :width].astype(jnp.float32)
    gates = jax.nn.sigmoid(glu_input[..., width:].astype(jnp.float32))
    gated = (values * gates).astype(jnp.bfloat16)
    padded = extended(gated, (("tensor", 1),), radius)
    conv_out = jnp.zeros(gated.shape, jnp.float32)
    for offset in range(taps):
        conv_out = conv_out + depth_kernel[offset] * padded[:, offset : offset + frames, :]
    mean_local = jnp.sum(conv_out, axis=(0, 1)) / local
    dev_local = conv_out - mean_local
    spread_local = jnp.sum(dev_local * dev_local, axis=(0, 1))
    if all(is_power_of_two(lax.axis_size(a)) for a in ("dp", "tensor")):
        average, spread = all_moments(mean_local, spread_local, float(local), ("dp", "tensor"))
        variance = spread / everyone
    else:
        average = lax.psum(jnp.sum(conv_out, axis=(0, 1)), ("dp", "tensor")) / everyone
        centred0 = conv_out - average
        variance = lax.psum(jnp.sum(centred0 * centred0, axis=(0, 1)), ("dp", "tensor")) / everyone
    own_columns = jnp.einsum("fd,cd->fc", group_grad, proj_weight, preferred_element_type=jnp.float32)
    grad_act = lax.all_to_all(own_columns, "tensor", split_axis=0, concat_axis=1, tiled=True)
    grad_act = grad_act.reshape(out_grad.shape)
    centred = conv_out - average
    inverse = lax.rsqrt(variance + epsilon)
    normed = centred * inverse
    affine = norm_scale * normed + norm_shift
    sig_affine = jax.nn.sigmoid(affine)
    activated = (affine * sig_affine).astype(jnp.bfloat16)
    flat_act = activated.reshape(-1, width)
    group_act = lax.all_to_all(flat_act, "tensor", split_axis=1, concat_axis=0, tiled=True)
    local_grad = jnp.einsum("fc,fd->cd", group_act, group_grad, preferred_element_type=jnp.float32)
    grad_affine = grad_act * (sig_affine + affine * sig_affine * (1.0 - sig_affine))
    sums = jnp.stack([jnp.sum(grad_affine, axis=(0, 1)), jnp.sum(grad_affine * normed, axis=(0, 1))])
    sums = all_sum(sums, ("dp", "tensor"))
    shift_grad, scale_grad = sums[0], sums[1]
    grad_conv = (
        norm_scale
        * inverse
        * (grad_affine - shift_grad / everyone - normed * scale_grad / everyone)
    ).astype(jnp.bfloat16)
    grad_pad = extended(grad_conv, (("tensor", 1),), radius)
    grad_gated = jnp.zeros(gated.shape, jnp.float32)
    for offset in range(taps):
        begin = 2 * radius - offset
        grad_gated = grad_gated + depth_kernel[offset] * grad_pad[:, begin : begin + frames, :]
    grad_wide = grad_conv.astype(jnp.float32)
    kernel_terms = jnp.stack(
        [
            jnp.sum(
                padded[:, offset : offset + frames, :].astype(jnp.float32) * grad_wide, axis=(0, 1)
            )
            for offset in range(taps)
        ]
    )
    weight_grad = rows_sum(local_grad, "dp")
    kernel_grad = all_sum(kernel_terms, ("dp", "tensor"))
    input_grad = jnp.concatenate(
        [grad_gated * gates, grad_gated * values * gates * (1.0 - gates)], axis=-1
    ).astype(jnp.bfloat16)
    full_weight = gather_weight(proj_weight)
    conv_output = jnp.einsum(
        "btc,cd->btd", activated, full_weight, preferred_element_type=jnp.float32
    ).astype(jnp.bfloat16)
    return (conv_output, input_grad, weight_grad, kernel_grad, scale_grad, shift_grad)


def solution(mesh):
    in_specs = (P("dp", "tensor", None), P(), P(), P(), P("tensor", None), P("dp", "tensor", None))
    out_specs = (P("dp", "tensor", None), P("dp", "tensor", None), P("tensor", None), P(), P(), P())
    return jax.shard_map(
        on_device, mesh=mesh, in_specs=in_specs, out_specs=out_specs, check_vma=False
    )
```

```python
import jax
import jax.numpy as jnp
from jax import lax
from jax.sharding import PartitionSpec as P

epsilon = 1e-05


def extended(array, sides, width):
    for axis, dim in sides:
        peers, length = (lax.axis_size(axis), array.shape[dim])
        up = [(i, (i + 1) % peers) for i in range(peers - 1)]
        down = [(j, i) for i, j in up]
        last = lax.slice_in_dim(array, length - width, length, axis=dim)
        leading = lax.slice_in_dim(array, 0, width, axis=dim)
        before = lax.ppermute(last, axis, up)
        after = lax.ppermute(leading, axis, down)
        array = jnp.concatenate([before, array, after], axis=dim)
    return array


def is_power_of_two(n):
    return n > 0 and (n & (n - 1)) == 0


def all_sum(x, axes):
    for axis in axes:
        peers = lax.axis_size(axis)
        if not is_power_of_two(peers):
            x = lax.psum(x, axis)
            continue
        step = 1
        while step < peers:
            x = x + lax.ppermute(x, axis, [(i, i ^ step) for i in range(peers)])
            step *= 2
    return x


def all_moments(mean, spread, count, axes):
    for axis in axes:
        peers = lax.axis_size(axis)
        step = 1
        while step < peers:
            other = lax.ppermute(jnp.stack([mean, spread]), axis, [(i, i ^ step) for i in range(peers)])
            delta = other[0] - mean
            mean = (mean + other[0]) * 0.5
            spread = (spread + other[1]) + delta * delta * (count * 0.5)
            count = count * 2
            step *= 2
    return mean, spread


def rows_sum(x, axis):
    peers = lax.axis_size(axis)
    if not is_power_of_two(peers) or x.shape[0] % peers:
        return lax.psum(x, axis)
    me = lax.axis_index(axis)
    bits = []
    step = 1
    while step < peers:
        bit = lax.rem(me // step, 2)
        half = x.shape[0] // 2
        keep = lax.dynamic_slice_in_dim(x, bit * half, half, axis=0)
        give = lax.dynamic_slice_in_dim(x, (1 - bit) * half, half, axis=0)
        x = keep + lax.ppermute(give, axis, [(i, i ^ step) for i in range(peers)])
        bits.append((step, bit))
        step *= 2
    for step, bit in reversed(bits):
        other = lax.ppermute(x, axis, [(i, i ^ step) for i in range(peers)])
        x = jnp.where(bit == 0, jnp.concatenate([x, other]), jnp.concatenate([other, x]))
    return x


def gather_weight(block):
    if lax.axis_size("dp") % 2:
        return lax.all_gather(block, "tensor", axis=0, tiled=True)
    peers = lax.axis_size("tensor")
    half = block.shape[0] // 2
    core = lax.rem(lax.axis_index("dp"), 2)
    mine = lax.dynamic_slice_in_dim(block, core * half, half, axis=0)
    held = lax.all_gather(mine, "tensor", axis=0, tiled=False)
    other = lax.ppermute(held, "dp", [(i, i ^ 1) for i in range(lax.axis_size("dp"))])
    first = jnp.where(core == 0, held, other)
    second = jnp.where(core == 0, other, held)
    return jnp.concatenate([first, second], axis=1).reshape(peers * block.shape[0], block.shape[1])


def on_device(glu_input, depth_kernel, norm_scale, norm_shift, proj_weight, out_grad):
    width = proj_weight.shape[1]
    rows = proj_weight.shape[0]
    frames = glu_input.shape[1]
    taps = depth_kernel.shape[0]
    radius = (taps - 1) // 2
    peers = lax.axis_size("tensor")
    me = lax.axis_index("tensor")
    local = glu_input.shape[0] * frames
    everyone = local * lax.axis_size("dp") * peers
    flat_grad = out_grad.reshape(-1, width)
    group_grad = lax.all_gather(flat_grad, "tensor", axis=0, tiled=True)
    values = glu_input[..., :width].astype(jnp.float32)
    gates = jax.nn.sigmoid(glu_input[..., width:].astype(jnp.float32))
    gated = (values * gates).astype(jnp.bfloat16)
    padded = extended(gated, (("tensor", 1),), radius)
    if frames >= 2 * radius:
        own = jnp.pad(gated, ((0, 0), (radius, radius), (0, 0)))
        conv_out = jnp.zeros(gated.shape, jnp.float32)
        for offset in range(taps):
            conv_out = conv_out + depth_kernel[offset] * own[:, offset : offset + frames, :]
        blank = jnp.zeros((gated.shape[0], 2 * radius, gated.shape[2]), gated.dtype)
        left = jnp.concatenate([padded[:, :radius], blank], axis=1)
        right = jnp.concatenate([blank, padded[:, frames + radius :]], axis=1)
        head = jnp.zeros((gated.shape[0], radius, gated.shape[2]), jnp.float32)
        tail = jnp.zeros((gated.shape[0], radius, gated.shape[2]), jnp.float32)
        for offset in range(taps):
            head = head + depth_kernel[offset] * left[:, offset : offset + radius, :]
            tail = tail + depth_kernel[offset] * right[:, offset : offset + radius, :]
        middle = jnp.zeros((gated.shape[0], frames - 2 * radius, gated.shape[2]), jnp.float32)
        conv_out = conv_out + jnp.concatenate([head, middle, tail], axis=1)
    else:
        conv_out = jnp.zeros(gated.shape, jnp.float32)
        for offset in range(taps):
            conv_out = conv_out + depth_kernel[offset] * padded[:, offset : offset + frames, :]
    mean_local = jnp.sum(conv_out, axis=(0, 1)) / local
    dev_local = conv_out - mean_local
    spread_local = jnp.sum(dev_local * dev_local, axis=(0, 1))
    if all(is_power_of_two(lax.axis_size(a)) for a in ("dp", "tensor")):
        average, spread = all_moments(mean_local, spread_local, float(local), ("dp", "tensor"))
        variance = spread / everyone
    else:
        average = lax.psum(jnp.sum(conv_out, axis=(0, 1)), ("dp", "tensor")) / everyone
        centred0 = conv_out - average
        variance = lax.psum(jnp.sum(centred0 * centred0, axis=(0, 1)), ("dp", "tensor")) / everyone
    group_grad, average = lax.optimization_barrier((group_grad, average))
    own_columns = jnp.einsum("fd,cd->fc", group_grad, proj_weight, preferred_element_type=jnp.float32)
    grad_act = lax.all_to_all(own_columns, "tensor", split_axis=0, concat_axis=1, tiled=True)
    grad_act = grad_act.reshape(out_grad.shape)
    centred = conv_out - average
    inverse = lax.rsqrt(variance + epsilon)
    normed = centred * inverse
    affine = norm_scale * normed + norm_shift
    sig_affine = jax.nn.sigmoid(affine)
    activated = (affine * sig_affine).astype(jnp.bfloat16)
    flat_act = activated.reshape(-1, width)
    group_act = lax.all_to_all(flat_act, "tensor", split_axis=1, concat_axis=0, tiled=True)
    local_grad = jnp.einsum("fc,fd->cd", group_act, group_grad, preferred_element_type=jnp.float32)
    grad_affine = grad_act * (sig_affine + affine * sig_affine * (1.0 - sig_affine))
    sums = jnp.stack([jnp.sum(grad_affine, axis=(0, 1)), jnp.sum(grad_affine * normed, axis=(0, 1))])
    sums = all_sum(sums, ("dp", "tensor"))
    shift_grad, scale_grad = sums[0], sums[1]
    grad_conv = (
        norm_scale
        * inverse
        * (grad_affine - shift_grad / everyone - normed * scale_grad / everyone)
    ).astype(jnp.bfloat16)
    grad_pad = extended(grad_conv, (("tensor", 1),), radius)
    grad_gated = jnp.zeros(gated.shape, jnp.float32)
    for offset in range(taps):
        begin = 2 * radius - offset
        grad_gated = grad_gated + depth_kernel[offset] * grad_pad[:, begin : begin + frames, :]
    grad_wide = grad_conv.astype(jnp.float32)
    kernel_terms = jnp.stack(
        [
            jnp.sum(
                padded[:, offset : offset + frames, :].astype(jnp.float32) * grad_wide, axis=(0, 1)
            )
            for offset in range(taps)
        ]
    )
    weight_grad = rows_sum(local_grad, "dp")
    kernel_grad = all_sum(kernel_terms, ("dp", "tensor"))
    input_grad = jnp.concatenate(
        [grad_gated * gates, grad_gated * values * gates * (1.0 - gates)], axis=-1
    ).astype(jnp.bfloat16)
    full_weight = gather_weight(proj_weight)
    conv_output = jnp.einsum(
        "btc,cd->btd", activated, full_weight, preferred_element_type=jnp.float32
    ).astype(jnp.bfloat16)
    return (conv_output, input_grad, weight_grad, kernel_grad, scale_grad, shift_grad)


def solution(mesh):
    in_specs = (P("dp", "tensor", None), P(), P(), P(), P("tensor", None), P("dp", "tensor", None))
    out_specs = (P("dp", "tensor", None), P("dp", "tensor", None), P("tensor", None), P(), P(), P())
    return jax.shard_map(
        on_device, mesh=mesh, in_specs=in_specs, out_specs=out_specs, check_vma=False
    )
```

```python
import jax
import jax.numpy as jnp
from jax import lax
from jax.sharding import PartitionSpec as P

epsilon = 1e-05


def extended(array, sides, width):
    for axis, dim in sides:
        peers, length = (lax.axis_size(axis), array.shape[dim])
        up = [(i, (i + 1) % peers) for i in range(peers - 1)]
        down = [(j, i) for i, j in up]
        last = lax.slice_in_dim(array, length - width, length, axis=dim)
        leading = lax.slice_in_dim(array, 0, width, axis=dim)
        before = lax.ppermute(last, axis, up)
        after = lax.ppermute(leading, axis, down)
        array = jnp.concatenate([before, array, after], axis=dim)
    return array


def is_power_of_two(n):
    return n > 0 and (n & (n - 1)) == 0


def all_sum(x, axes):
    for axis in axes:
        peers = lax.axis_size(axis)
        if not is_power_of_two(peers):
            x = lax.psum(x, axis)
            continue
        step = 1
        while step < peers:
            x = x + lax.ppermute(x, axis, [(i, i ^ step) for i in range(peers)])
            step *= 2
    return x


def all_moments(mean, spread, count, axes):
    for axis in axes:
        peers = lax.axis_size(axis)
        step = 1
        while step < peers:
            other = lax.ppermute(jnp.stack([mean, spread]), axis, [(i, i ^ step) for i in range(peers)])
            delta = other[0] - mean
            mean = (mean + other[0]) * 0.5
            spread = (spread + other[1]) + delta * delta * (count * 0.5)
            count = count * 2
            step *= 2
    return mean, spread


def rows_sum(x, axis):
    peers = lax.axis_size(axis)
    if not is_power_of_two(peers) or x.shape[0] % peers:
        return lax.psum(x, axis)
    me = lax.axis_index(axis)
    bits = []
    step = 1
    while step < peers:
        bit = lax.rem(me // step, 2)
        half = x.shape[0] // 2
        keep = lax.dynamic_slice_in_dim(x, bit * half, half, axis=0)
        give = lax.dynamic_slice_in_dim(x, (1 - bit) * half, half, axis=0)
        x = keep + lax.ppermute(give, axis, [(i, i ^ step) for i in range(peers)])
        bits.append((step, bit))
        step *= 2
    for step, bit in reversed(bits):
        other = lax.ppermute(x, axis, [(i, i ^ step) for i in range(peers)])
        x = jnp.where(bit == 0, jnp.concatenate([x, other]), jnp.concatenate([other, x]))
    return x


def gather_weight(block, anchor):
    if lax.axis_size("dp") % 2:
        return lax.all_gather(block, "tensor", axis=0, tiled=True), anchor
    peers = lax.axis_size("tensor")
    half = block.shape[0] // 2
    core = lax.rem(lax.axis_index("dp"), 2)
    mine = lax.dynamic_slice_in_dim(block, core * half, half, axis=0)
    held = lax.all_gather(mine, "tensor", axis=0, tiled=False)
    held, anchor = lax.optimization_barrier((held, anchor))
    other = lax.ppermute(held, "dp", [(i, i ^ 1) for i in range(lax.axis_size("dp"))])
    first = jnp.where(core == 0, held, other)
    second = jnp.where(core == 0, other, held)
    return jnp.concatenate([first, second], axis=1).reshape(peers * block.shape[0], block.shape[1]), anchor


def on_device(glu_input, depth_kernel, norm_scale, norm_shift, proj_weight, out_grad):
    width = proj_weight.shape[1]
    rows = proj_weight.shape[0]
    frames = glu_input.shape[1]
    taps = depth_kernel.shape[0]
    radius = (taps - 1) // 2
    peers = lax.axis_size("tensor")
    me = lax.axis_index("tensor")
    local = glu_input.shape[0] * frames
    everyone = local * lax.axis_size("dp") * peers
    flat_grad = out_grad.reshape(-1, width)
    group_grad = lax.all_gather(flat_grad, "tensor", axis=0, tiled=True)
    values = glu_input[..., :width].astype(jnp.float32)
    gates = jax.nn.sigmoid(glu_input[..., width:].astype(jnp.float32))
    gated = (values * gates).astype(jnp.bfloat16)
    padded = extended(gated, (("tensor", 1),), radius)
    conv_out = jnp.zeros(gated.shape, jnp.float32)
    for offset in range(taps):
        conv_out = conv_out + depth_kernel[offset] * padded[:, offset : offset + frames, :]
    mean_local = jnp.sum(conv_out, axis=(0, 1)) / local
    dev_local = conv_out - mean_local
    spread_local = jnp.sum(dev_local * dev_local, axis=(0, 1))
    if all(is_power_of_two(lax.axis_size(a)) for a in ("dp", "tensor")):
        average, spread = all_moments(mean_local, spread_local, float(local), ("dp", "tensor"))
        variance = spread / everyone
    else:
        average = lax.psum(jnp.sum(conv_out, axis=(0, 1)), ("dp", "tensor")) / everyone
        centred0 = conv_out - average
        variance = lax.psum(jnp.sum(centred0 * centred0, axis=(0, 1)), ("dp", "tensor")) / everyone
    group_grad, average = lax.optimization_barrier((group_grad, average))
    own_columns = jnp.einsum("fd,cd->fc", group_grad, proj_weight, preferred_element_type=jnp.float32)
    grad_act = lax.all_to_all(own_columns, "tensor", split_axis=0, concat_axis=1, tiled=True)
    grad_act = grad_act.reshape(out_grad.shape)
    centred = conv_out - average
    inverse = lax.rsqrt(variance + epsilon)
    normed = centred * inverse
    affine = norm_scale * normed + norm_shift
    sig_affine = jax.nn.sigmoid(affine)
    activated = (affine * sig_affine).astype(jnp.bfloat16)
    flat_act = activated.reshape(-1, width)
    group_act = lax.all_to_all(flat_act, "tensor", split_axis=1, concat_axis=0, tiled=True)
    local_grad = jnp.einsum("fc,fd->cd", group_act, group_grad, preferred_element_type=jnp.float32)
    grad_affine = grad_act * (sig_affine + affine * sig_affine * (1.0 - sig_affine))
    sums = jnp.stack([jnp.sum(grad_affine, axis=(0, 1)), jnp.sum(grad_affine * normed, axis=(0, 1))])
    sums = all_sum(sums, ("dp", "tensor"))
    shift_grad, scale_grad = sums[0], sums[1]
    grad_conv = (
        norm_scale
        * inverse
        * (grad_affine - shift_grad / everyone - normed * scale_grad / everyone)
    ).astype(jnp.bfloat16)
    grad_pad = extended(grad_conv, (("tensor", 1),), radius)
    grad_gated = jnp.zeros(gated.shape, jnp.float32)
    for offset in range(taps):
        begin = 2 * radius - offset
        grad_gated = grad_gated + depth_kernel[offset] * grad_pad[:, begin : begin + frames, :]
    grad_wide = grad_conv.astype(jnp.float32)
    kernel_terms = jnp.stack(
        [
            jnp.sum(
                padded[:, offset : offset + frames, :].astype(jnp.float32) * grad_wide, axis=(0, 1)
            )
            for offset in range(taps)
        ]
    )
    weight_grad = rows_sum(local_grad, "dp")
    kernel_grad = all_sum(kernel_terms, ("dp", "tensor"))
    input_grad = jnp.concatenate(
        [grad_gated * gates, grad_gated * values * gates * (1.0 - gates)], axis=-1
    ).astype(jnp.bfloat16)
    full_weight, kernel_grad = gather_weight(proj_weight, kernel_grad)
    conv_output = jnp.einsum(
        "btc,cd->btd", activated, full_weight, preferred_element_type=jnp.float32
    ).astype(jnp.bfloat16)
    return (conv_output, input_grad, weight_grad, kernel_grad, scale_grad, shift_grad)


def solution(mesh):
    in_specs = (P("dp", "tensor", None), P(), P(), P(), P("tensor", None), P("dp", "tensor", None))
    out_specs = (P("dp", "tensor", None), P("dp", "tensor", None), P("tensor", None), P(), P(), P())
    return jax.shard_map(
        on_device, mesh=mesh, in_specs=in_specs, out_specs=out_specs, check_vma=False
    )
```

```python
import jax
import jax.numpy as jnp
from jax import lax
from jax.sharding import PartitionSpec as P

epsilon = 1e-05


def extended(array, sides, width):
    for axis, dim in sides:
        peers, length = (lax.axis_size(axis), array.shape[dim])
        up = [(i, (i + 1) % peers) for i in range(peers - 1)]
        down = [(j, i) for i, j in up]
        last = lax.slice_in_dim(array, length - width, length, axis=dim)
        leading = lax.slice_in_dim(array, 0, width, axis=dim)
        before = lax.ppermute(last, axis, up)
        after = lax.ppermute(leading, axis, down)
        array = jnp.concatenate([before, array, after], axis=dim)
    return array


def is_power_of_two(n):
    return n > 0 and (n & (n - 1)) == 0


def all_sum(x, axes):
    for axis in axes:
        peers = lax.axis_size(axis)
        if not is_power_of_two(peers):
            x = lax.psum(x, axis)
            continue
        step = 1
        while step < peers:
            x = x + lax.ppermute(x, axis, [(i, i ^ step) for i in range(peers)])
            step *= 2
    return x


def all_moments(mean, spread, count, axes):
    for axis in axes:
        peers = lax.axis_size(axis)
        step = 1
        while step < peers:
            other = lax.ppermute(jnp.stack([mean, spread]), axis, [(i, i ^ step) for i in range(peers)])
            delta = other[0] - mean
            mean = (mean + other[0]) * 0.5
            spread = (spread + other[1]) + delta * delta * (count * 0.5)
            count = count * 2
            step *= 2
    return mean, spread


def rows_sum(x, axis):
    peers = lax.axis_size(axis)
    if not is_power_of_two(peers) or x.shape[0] % peers:
        return lax.psum(x, axis)
    me = lax.axis_index(axis)
    bits = []
    step = 1
    while step < peers:
        bit = lax.rem(me // step, 2)
        half = x.shape[0] // 2
        keep = lax.dynamic_slice_in_dim(x, bit * half, half, axis=0)
        give = lax.dynamic_slice_in_dim(x, (1 - bit) * half, half, axis=0)
        x = keep + lax.ppermute(give, axis, [(i, i ^ step) for i in range(peers)])
        bits.append((step, bit))
        step *= 2
    for step, bit in reversed(bits):
        other = lax.ppermute(x, axis, [(i, i ^ step) for i in range(peers)])
        x = jnp.where(bit == 0, jnp.concatenate([x, other]), jnp.concatenate([other, x]))
    return x


def gather_weight(block, anchor):
    if lax.axis_size("dp") % 2:
        return lax.all_gather(block, "tensor", axis=0, tiled=True), anchor
    peers = lax.axis_size("tensor")
    half = block.shape[0] // 2
    core = lax.rem(lax.axis_index("dp"), 2)
    mine = lax.dynamic_slice_in_dim(block, core * half, half, axis=0)
    held = lax.all_gather(mine, "tensor", axis=0, tiled=False)
    held, anchor = lax.optimization_barrier((held, anchor))
    other = lax.ppermute(held, "dp", [(i, i ^ 1) for i in range(lax.axis_size("dp"))])
    first = jnp.where(core == 0, held, other)
    second = jnp.where(core == 0, other, held)
    return jnp.concatenate([first, second], axis=1).reshape(peers * block.shape[0], block.shape[1]), anchor


def on_device(glu_input, depth_kernel, norm_scale, norm_shift, proj_weight, out_grad):
    width = proj_weight.shape[1]
    rows = proj_weight.shape[0]
    frames = glu_input.shape[1]
    taps = depth_kernel.shape[0]
    radius = (taps - 1) // 2
    peers = lax.axis_size("tensor")
    me = lax.axis_index("tensor")
    local = glu_input.shape[0] * frames
    everyone = local * lax.axis_size("dp") * peers
    flat_grad = out_grad.reshape(-1, width)
    group_grad = lax.all_gather(flat_grad, "tensor", axis=0, tiled=True)
    values = glu_input[..., :width].astype(jnp.float32)
    gates = jax.nn.sigmoid(glu_input[..., width:].astype(jnp.float32))
    gated = (values * gates).astype(jnp.bfloat16)
    padded = extended(gated, (("tensor", 1),), radius)
    conv_out = jnp.zeros(gated.shape, jnp.float32)
    for offset in range(taps):
        conv_out = conv_out + depth_kernel[offset] * padded[:, offset : offset + frames, :]
    mean_local = jnp.sum(conv_out, axis=(0, 1)) / local
    dev_local = conv_out - mean_local
    spread_local = jnp.sum(dev_local * dev_local, axis=(0, 1))
    if all(is_power_of_two(lax.axis_size(a)) for a in ("dp", "tensor")):
        average, spread = all_moments(mean_local, spread_local, float(local), ("dp", "tensor"))
        variance = spread / everyone
    else:
        average = lax.psum(jnp.sum(conv_out, axis=(0, 1)), ("dp", "tensor")) / everyone
        centred0 = conv_out - average
        variance = lax.psum(jnp.sum(centred0 * centred0, axis=(0, 1)), ("dp", "tensor")) / everyone
    group_grad, average = lax.optimization_barrier((group_grad, average))
    own_columns = jnp.einsum("fd,cd->fc", group_grad, proj_weight, preferred_element_type=jnp.float32)
    grad_act = lax.all_to_all(own_columns, "tensor", split_axis=0, concat_axis=1, tiled=True)
    grad_act = grad_act.reshape(out_grad.shape)
    centred = conv_out - average
    inverse = lax.rsqrt(variance + epsilon)
    normed = centred * inverse
    affine = norm_scale * normed + norm_shift
    sig_affine = jax.nn.sigmoid(affine)
    activated = (affine * sig_affine).astype(jnp.bfloat16)
    flat_act = activated.reshape(-1, width)
    group_act = lax.all_to_all(flat_act, "tensor", split_axis=1, concat_axis=0, tiled=True)
    local_grad = jnp.einsum("fc,fd->cd", group_act, group_grad, preferred_element_type=jnp.float32)
    grad_affine = grad_act * (sig_affine + affine * sig_affine * (1.0 - sig_affine))
    sums = jnp.stack([jnp.sum(grad_affine, axis=(0, 1)), jnp.sum(grad_affine * normed, axis=(0, 1))])
    sums = all_sum(sums, ("dp", "tensor"))
    full_weight, sums = gather_weight(proj_weight, sums)
    shift_grad, scale_grad = sums[0], sums[1]
    grad_conv = (
        norm_scale
        * inverse
        * (grad_affine - shift_grad / everyone - normed * scale_grad / everyone)
    ).astype(jnp.bfloat16)
    grad_pad = extended(grad_conv, (("tensor", 1),), radius)
    grad_gated = jnp.zeros(gated.shape, jnp.float32)
    for offset in range(taps):
        begin = 2 * radius - offset
        grad_gated = grad_gated + depth_kernel[offset] * grad_pad[:, begin : begin + frames, :]
    grad_wide = grad_conv.astype(jnp.float32)
    kernel_terms = jnp.stack(
        [
            jnp.sum(
                padded[:, offset : offset + frames, :].astype(jnp.float32) * grad_wide, axis=(0, 1)
            )
            for offset in range(taps)
        ]
    )
    weight_grad = rows_sum(local_grad, "dp")
    kernel_grad = all_sum(kernel_terms, ("dp", "tensor"))
    input_grad = jnp.concatenate(
        [grad_gated * gates, grad_gated * values * gates * (1.0 - gates)], axis=-1
    ).astype(jnp.bfloat16)
    conv_output = jnp.einsum(
        "btc,cd->btd", activated, full_weight, preferred_element_type=jnp.float32
    ).astype(jnp.bfloat16)
    return (conv_output, input_grad, weight_grad, kernel_grad, scale_grad, shift_grad)


def solution(mesh):
    in_specs = (P("dp", "tensor", None), P(), P(), P(), P("tensor", None), P("dp", "tensor", None))
    out_specs = (P("dp", "tensor", None), P("dp", "tensor", None), P("tensor", None), P(), P(), P())
    return jax.shard_map(
        on_device, mesh=mesh, in_specs=in_specs, out_specs=out_specs, check_vma=False
    )
```

```python
import jax
import jax.numpy as jnp
from jax import lax
from jax.sharding import PartitionSpec as P

epsilon = 1e-05


def extended(array, sides, width):
    for axis, dim in sides:
        peers, length = (lax.axis_size(axis), array.shape[dim])
        up = [(i, (i + 1) % peers) for i in range(peers - 1)]
        down = [(j, i) for i, j in up]
        last = lax.slice_in_dim(array, length - width, length, axis=dim)
        leading = lax.slice_in_dim(array, 0, width, axis=dim)
        before = lax.ppermute(last, axis, up)
        after = lax.ppermute(leading, axis, down)
        array = jnp.concatenate([before, array, after], axis=dim)
    return array


def is_power_of_two(n):
    return n > 0 and (n & (n - 1)) == 0


def all_sum(x, axes):
    for axis in axes:
        peers = lax.axis_size(axis)
        if not is_power_of_two(peers):
            x = lax.psum(x, axis)
            continue
        step = 1
        while step < peers:
            x = x + lax.ppermute(x, axis, [(i, i ^ step) for i in range(peers)])
            step *= 2
    return x


def all_moments(mean, spread, count, axes):
    for axis in axes:
        peers = lax.axis_size(axis)
        step = 1
        while step < peers:
            other = lax.ppermute(jnp.stack([mean, spread]), axis, [(i, i ^ step) for i in range(peers)])
            delta = other[0] - mean
            mean = (mean + other[0]) * 0.5
            spread = (spread + other[1]) + delta * delta * (count * 0.5)
            count = count * 2
            step *= 2
    return mean, spread


def rows_sum(x, axis):
    peers = lax.axis_size(axis)
    if not is_power_of_two(peers) or x.shape[0] % peers:
        return lax.psum(x, axis)
    me = lax.axis_index(axis)
    bits = []
    step = 1
    while step < peers:
        bit = lax.rem(me // step, 2)
        half = x.shape[0] // 2
        keep = lax.dynamic_slice_in_dim(x, bit * half, half, axis=0)
        give = lax.dynamic_slice_in_dim(x, (1 - bit) * half, half, axis=0)
        x = keep + lax.ppermute(give, axis, [(i, i ^ step) for i in range(peers)])
        bits.append((step, bit))
        step *= 2
    for step, bit in reversed(bits):
        other = lax.ppermute(x, axis, [(i, i ^ step) for i in range(peers)])
        x = jnp.where(bit == 0, jnp.concatenate([x, other]), jnp.concatenate([other, x]))
    return x


def gather_weight(block):
    if lax.axis_size("dp") % 2:
        return lax.all_gather(block, "tensor", axis=0, tiled=True)
    peers = lax.axis_size("tensor")
    half = block.shape[0] // 2
    core = lax.rem(lax.axis_index("dp"), 2)
    mine = lax.dynamic_slice_in_dim(block, core * half, half, axis=0)
    held = lax.all_gather(mine, "tensor", axis=0, tiled=False)
    other = lax.ppermute(held, "dp", [(i, i ^ 1) for i in range(lax.axis_size("dp"))])
    first = jnp.where(core == 0, held, other)
    second = jnp.where(core == 0, other, held)
    return jnp.concatenate([first, second], axis=1).reshape(peers * block.shape[0], block.shape[1])


def on_device(glu_input, depth_kernel, norm_scale, norm_shift, proj_weight, out_grad):
    width = proj_weight.shape[1]
    rows = proj_weight.shape[0]
    frames = glu_input.shape[1]
    taps = depth_kernel.shape[0]
    radius = (taps - 1) // 2
    peers = lax.axis_size("tensor")
    me = lax.axis_index("tensor")
    local = glu_input.shape[0] * frames
    everyone = local * lax.axis_size("dp") * peers
    flat_grad = out_grad.reshape(-1, width)
    group_grad = lax.all_gather(flat_grad, "tensor", axis=0, tiled=True)
    values = glu_input[..., :width].astype(jnp.float32)
    gates = jax.nn.sigmoid(glu_input[..., width:].astype(jnp.float32))
    gated = (values * gates).astype(jnp.bfloat16)
    padded = extended(gated, (("tensor", 1),), radius)
    conv_out = jnp.zeros(gated.shape, jnp.float32)
    for offset in range(taps):
        conv_out = conv_out + depth_kernel[offset] * padded[:, offset : offset + frames, :]
    mean_local = jnp.sum(conv_out, axis=(0, 1)) / local
    dev_local = conv_out - mean_local
    spread_local = jnp.sum(dev_local * dev_local, axis=(0, 1))
    if all(is_power_of_two(lax.axis_size(a)) for a in ("dp", "tensor")):
        average, spread = all_moments(mean_local, spread_local, float(local), ("dp", "tensor"))
        variance = spread / everyone
    else:
        average = lax.psum(jnp.sum(conv_out, axis=(0, 1)), ("dp", "tensor")) / everyone
        centred0 = conv_out - average
        variance = lax.psum(jnp.sum(centred0 * centred0, axis=(0, 1)), ("dp", "tensor")) / everyone
    group_grad, average = lax.optimization_barrier((group_grad, average))
    own_columns = jnp.einsum("fd,cd->fc", group_grad, proj_weight, preferred_element_type=jnp.float32)
    grad_act = lax.all_to_all(own_columns, "tensor", split_axis=0, concat_axis=1, tiled=True)
    grad_act = grad_act.reshape(out_grad.shape)
    centred = conv_out - average
    inverse = lax.rsqrt(variance + epsilon)
    normed = centred * inverse
    affine = norm_scale * normed + norm_shift
    sig_affine = jax.nn.sigmoid(affine)
    activated = (affine * sig_affine).astype(jnp.bfloat16)
    flat_act = activated.reshape(-1, width)
    group_act = lax.all_to_all(flat_act, "tensor", split_axis=1, concat_axis=0, tiled=True)
    local_grad = jnp.einsum("fc,fd->cd", group_act, group_grad, preferred_element_type=jnp.float32)
    grad_affine = grad_act * (sig_affine + affine * sig_affine * (1.0 - sig_affine))
    sums = jnp.stack([jnp.sum(grad_affine, axis=(0, 1)), jnp.sum(grad_affine * normed, axis=(0, 1))])
    sums = all_sum(sums, ("dp", "tensor"))
    shift_grad, scale_grad = sums[0], sums[1]
    grad_conv = (
        norm_scale
        * inverse
        * (grad_affine - shift_grad / everyone - normed * scale_grad / everyone)
    ).astype(jnp.bfloat16)
    grad_pad = extended(grad_conv, (("tensor", 1),), radius)
    grad_gated = jnp.zeros(gated.shape, jnp.float32)
    for offset in range(taps):
        begin = 2 * radius - offset
        grad_gated = grad_gated + depth_kernel[offset] * grad_pad[:, begin : begin + frames, :]
    grad_wide = grad_conv.astype(jnp.float32)
    kernel_terms = jnp.stack(
        [
            jnp.sum(
                padded[:, offset : offset + frames, :].astype(jnp.float32) * grad_wide, axis=(0, 1)
            )
            for offset in range(taps)
        ]
    )
    weight_grad = rows_sum(local_grad, "dp")
    kernel_grad = all_sum(kernel_terms, ("tensor", "dp"))
    input_grad = jnp.concatenate(
        [grad_gated * gates, grad_gated * values * gates * (1.0 - gates)], axis=-1
    ).astype(jnp.bfloat16)
    full_weight = gather_weight(proj_weight)
    conv_output = jnp.einsum(
        "btc,cd->btd", activated, full_weight, preferred_element_type=jnp.float32
    ).astype(jnp.bfloat16)
    return (conv_output, input_grad, weight_grad, kernel_grad, scale_grad, shift_grad)


def solution(mesh):
    in_specs = (P("dp", "tensor", None), P(), P(), P(), P("tensor", None), P("dp", "tensor", None))
    out_specs = (P("dp", "tensor", None), P("dp", "tensor", None), P("tensor", None), P(), P(), P())
    return jax.shard_map(
        on_device, mesh=mesh, in_specs=in_specs, out_specs=out_specs, check_vma=False
    )
```

```python
import jax
import jax.numpy as jnp
from jax import lax
from jax.sharding import PartitionSpec as P

epsilon = 1e-05


def extended(array, sides, width):
    for axis, dim in sides:
        peers, length = (lax.axis_size(axis), array.shape[dim])
        up = [(i, (i + 1) % peers) for i in range(peers - 1)]
        down = [(j, i) for i, j in up]
        last = lax.slice_in_dim(array, length - width, length, axis=dim)
        leading = lax.slice_in_dim(array, 0, width, axis=dim)
        before = lax.ppermute(last, axis, up)
        after = lax.ppermute(leading, axis, down)
        array = jnp.concatenate([before, array, after], axis=dim)
    return array


def is_power_of_two(n):
    return n > 0 and (n & (n - 1)) == 0


def all_sum(x, axes):
    for axis in axes:
        peers = lax.axis_size(axis)
        if not is_power_of_two(peers):
            x = lax.psum(x, axis)
            continue
        step = 1
        while step < peers:
            x = x + lax.ppermute(x, axis, [(i, i ^ step) for i in range(peers)])
            step *= 2
    return x


def all_moments(mean, spread, count, axes):
    for axis in axes:
        peers = lax.axis_size(axis)
        step = 1
        while step < peers:
            other = lax.ppermute(jnp.stack([mean, spread]), axis, [(i, i ^ step) for i in range(peers)])
            delta = other[0] - mean
            mean = (mean + other[0]) * 0.5
            spread = (spread + other[1]) + delta * delta * (count * 0.5)
            count = count * 2
            step *= 2
    return mean, spread


def rows_sum(x, axis):
    peers = lax.axis_size(axis)
    if not is_power_of_two(peers) or x.shape[0] % peers:
        return lax.psum(x, axis)
    me = lax.axis_index(axis)
    bits = []
    step = peers // 2
    while step >= 1:
        bit = lax.rem(me // step, 2)
        half = x.shape[0] // 2
        keep = lax.dynamic_slice_in_dim(x, bit * half, half, axis=0)
        give = lax.dynamic_slice_in_dim(x, (1 - bit) * half, half, axis=0)
        x = keep + lax.ppermute(give, axis, [(i, i ^ step) for i in range(peers)])
        bits.append((step, bit))
        step //= 2
    for step, bit in reversed(bits):
        other = lax.ppermute(x, axis, [(i, i ^ step) for i in range(peers)])
        x = jnp.where(bit == 0, jnp.concatenate([x, other]), jnp.concatenate([other, x]))
    return x


def gather_weight(block):
    if lax.axis_size("dp") % 2:
        return lax.all_gather(block, "tensor", axis=0, tiled=True)
    peers = lax.axis_size("tensor")
    half = block.shape[0] // 2
    core = lax.rem(lax.axis_index("dp"), 2)
    mine = lax.dynamic_slice_in_dim(block, core * half, half, axis=0)
    held = lax.all_gather(mine, "tensor", axis=0, tiled=False)
    other = lax.ppermute(held, "dp", [(i, i ^ 1) for i in range(lax.axis_size("dp"))])
    first = jnp.where(core == 0, held, other)
    second = jnp.where(core == 0, other, held)
    return jnp.concatenate([first, second], axis=1).reshape(peers * block.shape[0], block.shape[1])


def on_device(glu_input, depth_kernel, norm_scale, norm_shift, proj_weight, out_grad):
    width = proj_weight.shape[1]
    rows = proj_weight.shape[0]
    frames = glu_input.shape[1]
    taps = depth_kernel.shape[0]
    radius = (taps - 1) // 2
    peers = lax.axis_size("tensor")
    me = lax.axis_index("tensor")
    local = glu_input.shape[0] * frames
    everyone = local * lax.axis_size("dp") * peers
    flat_grad = out_grad.reshape(-1, width)
    group_grad = lax.all_gather(flat_grad, "tensor", axis=0, tiled=True)
    values = glu_input[..., :width].astype(jnp.float32)
    gates = jax.nn.sigmoid(glu_input[..., width:].astype(jnp.float32))
    gated = (values * gates).astype(jnp.bfloat16)
    padded = extended(gated, (("tensor", 1),), radius)
    conv_out = jnp.zeros(gated.shape, jnp.float32)
    for offset in range(taps):
        conv_out = conv_out + depth_kernel[offset] * padded[:, offset : offset + frames, :]
    mean_local = jnp.sum(conv_out, axis=(0, 1)) / local
    dev_local = conv_out - mean_local
    spread_local = jnp.sum(dev_local * dev_local, axis=(0, 1))
    if all(is_power_of_two(lax.axis_size(a)) for a in ("dp", "tensor")):
        average, spread = all_moments(mean_local, spread_local, float(local), ("dp", "tensor"))
        variance = spread / everyone
    else:
        average = lax.psum(jnp.sum(conv_out, axis=(0, 1)), ("dp", "tensor")) / everyone
        centred0 = conv_out - average
        variance = lax.psum(jnp.sum(centred0 * centred0, axis=(0, 1)), ("dp", "tensor")) / everyone
    group_grad, average = lax.optimization_barrier((group_grad, average))
    own_columns = jnp.einsum("fd,cd->fc", group_grad, proj_weight, preferred_element_type=jnp.float32)
    grad_act = lax.all_to_all(own_columns, "tensor", split_axis=0, concat_axis=1, tiled=True)
    grad_act = grad_act.reshape(out_grad.shape)
    centred = conv_out - average
    inverse = lax.rsqrt(variance + epsilon)
    normed = centred * inverse
    affine = norm_scale * normed + norm_shift
    sig_affine = jax.nn.sigmoid(affine)
    activated = (affine * sig_affine).astype(jnp.bfloat16)
    flat_act = activated.reshape(-1, width)
    group_act = lax.all_to_all(flat_act, "tensor", split_axis=1, concat_axis=0, tiled=True)
    local_grad = jnp.einsum("fc,fd->cd", group_act, group_grad, preferred_element_type=jnp.float32)
    grad_affine = grad_act * (sig_affine + affine * sig_affine * (1.0 - sig_affine))
    sums = jnp.stack([jnp.sum(grad_affine, axis=(0, 1)), jnp.sum(grad_affine * normed, axis=(0, 1))])
    sums = all_sum(sums, ("dp", "tensor"))
    shift_grad, scale_grad = sums[0], sums[1]
    grad_conv = (
        norm_scale
        * inverse
        * (grad_affine - shift_grad / everyone - normed * scale_grad / everyone)
    ).astype(jnp.bfloat16)
    grad_pad = extended(grad_conv, (("tensor", 1),), radius)
    grad_gated = jnp.zeros(gated.shape, jnp.float32)
    for offset in range(taps):
        begin = 2 * radius - offset
        grad_gated = grad_gated + depth_kernel[offset] * grad_pad[:, begin : begin + frames, :]
    grad_wide = grad_conv.astype(jnp.float32)
    kernel_terms = jnp.stack(
        [
            jnp.sum(
                padded[:, offset : offset + frames, :].astype(jnp.float32) * grad_wide, axis=(0, 1)
            )
            for offset in range(taps)
        ]
    )
    weight_grad = rows_sum(local_grad, "dp")
    kernel_grad = all_sum(kernel_terms, ("dp", "tensor"))
    input_grad = jnp.concatenate(
        [grad_gated * gates, grad_gated * values * gates * (1.0 - gates)], axis=-1
    ).astype(jnp.bfloat16)
    full_weight = gather_weight(proj_weight)
    conv_output = jnp.einsum(
        "btc,cd->btd", activated, full_weight, preferred_element_type=jnp.float32
    ).astype(jnp.bfloat16)
    return (conv_output, input_grad, weight_grad, kernel_grad, scale_grad, shift_grad)


def solution(mesh):
    in_specs = (P("dp", "tensor", None), P(), P(), P(), P("tensor", None), P("dp", "tensor", None))
    out_specs = (P("dp", "tensor", None), P("dp", "tensor", None), P("tensor", None), P(), P(), P())
    return jax.shard_map(
        on_device, mesh=mesh, in_specs=in_specs, out_specs=out_specs, check_vma=False
    )
```

```python
import jax
import jax.numpy as jnp
from jax import lax
from jax.sharding import PartitionSpec as P

epsilon = 1e-05


def extended(array, sides, width):
    for axis, dim in sides:
        peers, length = (lax.axis_size(axis), array.shape[dim])
        up = [(i, (i + 1) % peers) for i in range(peers - 1)]
        down = [(j, i) for i, j in up]
        last = lax.slice_in_dim(array, length - width, length, axis=dim)
        leading = lax.slice_in_dim(array, 0, width, axis=dim)
        before = lax.ppermute(last, axis, up)
        after = lax.ppermute(leading, axis, down)
        array = jnp.concatenate([before, array, after], axis=dim)
    return array


def is_power_of_two(n):
    return n > 0 and (n & (n - 1)) == 0


def all_sum(x, axes):
    for axis in axes:
        peers = lax.axis_size(axis)
        if not is_power_of_two(peers):
            x = lax.psum(x, axis)
            continue
        step = 1
        while step < peers:
            x = x + lax.ppermute(x, axis, [(i, i ^ step) for i in range(peers)])
            step *= 2
    return x


def all_moments(mean, spread, count, axes):
    for axis in axes:
        peers = lax.axis_size(axis)
        step = 1
        while step < peers:
            other = lax.ppermute(jnp.stack([mean, spread]), axis, [(i, i ^ step) for i in range(peers)])
            delta = other[0] - mean
            mean = (mean + other[0]) * 0.5
            spread = (spread + other[1]) + delta * delta * (count * 0.5)
            count = count * 2
            step *= 2
    return mean, spread


def rows_sum(x, axis):
    peers = lax.axis_size(axis)
    if not is_power_of_two(peers) or x.shape[0] % peers:
        return lax.psum(x, axis)
    me = lax.axis_index(axis)
    bits = []
    step = 1
    while step < peers:
        bit = lax.rem(me // step, 2)
        half = x.shape[0] // 2
        keep = lax.dynamic_slice_in_dim(x, bit * half, half, axis=0)
        give = lax.dynamic_slice_in_dim(x, (1 - bit) * half, half, axis=0)
        x = keep + lax.ppermute(give, axis, [(i, i ^ step) for i in range(peers)])
        bits.append((step, bit))
        step *= 2
    for step, bit in reversed(bits):
        other = lax.ppermute(x, axis, [(i, i ^ step) for i in range(peers)])
        x = jnp.where(bit == 0, jnp.concatenate([x, other]), jnp.concatenate([other, x]))
    return x


def gather_weight(block):
    if lax.axis_size("dp") % 2:
        return lax.all_gather(block, "tensor", axis=0, tiled=True)
    peers = lax.axis_size("tensor")
    half = block.shape[0] // 2
    core = lax.rem(lax.axis_index("dp"), 2)
    mine = lax.dynamic_slice_in_dim(block, core * half, half, axis=0)
    held = lax.all_gather(mine, "tensor", axis=0, tiled=False)
    other = lax.ppermute(held, "dp", [(i, i ^ 1) for i in range(lax.axis_size("dp"))])
    first = jnp.where(core == 0, held, other)
    second = jnp.where(core == 0, other, held)
    return jnp.concatenate([first, second], axis=1).reshape(peers * block.shape[0], block.shape[1])


def on_device(glu_input, depth_kernel, norm_scale, norm_shift, proj_weight, out_grad):
    width = proj_weight.shape[1]
    rows = proj_weight.shape[0]
    frames = glu_input.shape[1]
    taps = depth_kernel.shape[0]
    radius = (taps - 1) // 2
    peers = lax.axis_size("tensor")
    me = lax.axis_index("tensor")
    local = glu_input.shape[0] * frames
    everyone = local * lax.axis_size("dp") * peers
    flat_grad = out_grad.reshape(-1, width)
    group_grad = lax.all_gather(flat_grad, "tensor", axis=0, tiled=True)
    values = glu_input[..., :width].astype(jnp.float32)
    gates = jax.nn.sigmoid(glu_input[..., width:].astype(jnp.float32))
    gated = (values * gates).astype(jnp.bfloat16)
    padded = extended(gated, (("tensor", 1),), radius)
    conv_out = jnp.zeros(gated.shape, jnp.float32)
    for offset in range(taps):
        conv_out = conv_out + depth_kernel[offset] * padded[:, offset : offset + frames, :]
    mean_local = jnp.sum(conv_out, axis=(0, 1)) / local
    dev_local = conv_out - mean_local
    spread_local = jnp.sum(dev_local * dev_local, axis=(0, 1))
    if all(is_power_of_two(lax.axis_size(a)) for a in ("dp", "tensor")):
        average, spread = all_moments(mean_local, spread_local, float(local), ("dp", "tensor"))
        variance = spread / everyone
    else:
        average = lax.psum(jnp.sum(conv_out, axis=(0, 1)), ("dp", "tensor")) / everyone
        centred0 = conv_out - average
        variance = lax.psum(jnp.sum(centred0 * centred0, axis=(0, 1)), ("dp", "tensor")) / everyone
    group_grad, average = lax.optimization_barrier((group_grad, average))
    own_columns = jnp.einsum("fd,cd->fc", group_grad, proj_weight, preferred_element_type=jnp.float32)
    grad_act = lax.all_to_all(own_columns, "tensor", split_axis=0, concat_axis=1, tiled=True)
    grad_act = grad_act.reshape(out_grad.shape)
    centred = conv_out - average
    inverse = lax.rsqrt(variance + epsilon)
    normed = centred * inverse
    affine = norm_scale * normed + norm_shift
    sig_affine = jax.nn.sigmoid(affine)
    activated = (affine * sig_affine).astype(jnp.bfloat16)
    flat_act = activated.reshape(-1, width)
    group_act = lax.all_to_all(flat_act, "tensor", split_axis=1, concat_axis=0, tiled=True)
    local_grad = jnp.einsum("fc,fd->cd", group_act, group_grad, preferred_element_type=jnp.float32)
    grad_affine = grad_act * (sig_affine + affine * sig_affine * (1.0 - sig_affine))
    sums = jnp.stack([jnp.sum(grad_affine, axis=(0, 1)), jnp.sum(grad_affine * normed, axis=(0, 1))])
    sums = all_sum(sums, ("tensor", "dp"))
    shift_grad, scale_grad = sums[0], sums[1]
    grad_conv = (
        norm_scale
        * inverse
        * (grad_affine - shift_grad / everyone - normed * scale_grad / everyone)
    ).astype(jnp.bfloat16)
    grad_pad = extended(grad_conv, (("tensor", 1),), radius)
    grad_gated = jnp.zeros(gated.shape, jnp.float32)
    for offset in range(taps):
        begin = 2 * radius - offset
        grad_gated = grad_gated + depth_kernel[offset] * grad_pad[:, begin : begin + frames, :]
    grad_wide = grad_conv.astype(jnp.float32)
    kernel_terms = jnp.stack(
        [
            jnp.sum(
                padded[:, offset : offset + frames, :].astype(jnp.float32) * grad_wide, axis=(0, 1)
            )
            for offset in range(taps)
        ]
    )
    weight_grad = rows_sum(local_grad, "dp")
    kernel_grad = all_sum(kernel_terms, ("dp", "tensor"))
    input_grad = jnp.concatenate(
        [grad_gated * gates, grad_gated * values * gates * (1.0 - gates)], axis=-1
    ).astype(jnp.bfloat16)
    full_weight = gather_weight(proj_weight)
    conv_output = jnp.einsum(
        "btc,cd->btd", activated, full_weight, preferred_element_type=jnp.float32
    ).astype(jnp.bfloat16)
    return (conv_output, input_grad, weight_grad, kernel_grad, scale_grad, shift_grad)


def solution(mesh):
    in_specs = (P("dp", "tensor", None), P(), P(), P(), P("tensor", None), P("dp", "tensor", None))
    out_specs = (P("dp", "tensor", None), P("dp", "tensor", None), P("tensor", None), P(), P(), P())
    return jax.shard_map(
        on_device, mesh=mesh, in_specs=in_specs, out_specs=out_specs, check_vma=False
    )
```
